256 devices in a mesh: req: 64 (over y, z, core), tp: 4 (over x).
Axes of the slice: x: 4, y: 4, z: 8, core: 2. Of those that a mesh axis runs over, the one named last changes fastest.
Arguments:
- queries: bfloat16 [64, 1280, 24, 128], P('req', None, 'tp'), may hold values from -25 to 25
- text_kv: bfloat16 [64, 1280, 4, 256], P('req', None, 'tp'), may hold values from -6 to 6
- image_rows: bfloat16 [32768, 6144], P('req', 'tp'), may hold values from -6 to 6
- row_request: int32 [32768], P('req'), may hold values from 0 to 63, as said below
- row_position: int32 [32768], P('req'), may hold values from 8 to 1263, as said below
- prompt_lengths: int32 [64], P('req'), may hold values from 24 to 1280, as said below
- kv_weight: bfloat16 [6144, 4, 256], P('tp'), may hold values from -0.078125 to 0.078125
Outputs:
- attended: bfloat16 [64, 1280, 24, 128], P('req', None, 'tp')
The draws below stay inside these ranges and needn't reach their ends.
Inputs may be any that keep to these rules, and one draw needn't show every extreme that they name: `row_request`: the rows of one device name one request at most 16 times, and on every device some request is named exactly 16 times. `row_position`: the rows naming one request take distinct positions, 8 or more, that form one run ending at least 16 positions before that request's length. `prompt_lengths`: some request has length exactly 1280.
All inputs are finite; a program needn't handle non-finite values.
Results may differ from the reference program's by a relative error of at most 0.0085.
Values may be sent and summed in bfloat16 or wider, within the bound.
No kernel may reach another device: no remote copies, remote signals or barrier semaphores. Data moves between devices by JAX's collectives and lax.ppermute only.
A program may use at most 128 MiB of HBM per device.

```python
import math
import jax
import jax.numpy as jnp
from jax import lax

D = 6144
HD = 128
QH = 24
KVH = 4
PROMPT = 1280
IMG_DEV = 512
REQS = 64
IMG_ROWS = 32768
CAP = 16


def layout(key):
    key_caps, key_first, key_noise, key_order, key_offset, key_tail = jax.random.split(jax.random.fold_in(key, 5), 6)
    total = REQS * CAP
    per_cap = jax.random.randint(key_caps, (REQS,), CAP // 2, CAP + 1)
    forced_req = jax.random.randint(key_first, (REQS,), 0, REQS)
    slot_req = jnp.arange(total, dtype=jnp.int32) // CAP
    slot_num = jnp.arange(total, dtype=jnp.int32) % CAP
    noise = jax.random.randint(key_noise, (REQS, total), 1, 2 ** 20 - 1)
    live = slot_num[None, :] < per_cap[slot_req][None, :]
    forced = slot_req[None, :] == forced_req[:, None]
    score = jnp.where(forced, 0, jnp.where(live, noise, 2 ** 20 - 1))
    score = score * total + jnp.arange(total, dtype=jnp.int32)[None, :]
    chosen = jnp.argsort(score, axis=1)[:, :IMG_DEV]
    dest = slot_req[chosen]
    shuffle_key = jax.random.randint(key_order, (REQS, IMG_DEV), 0, 2 ** 20) * IMG_DEV + jnp.arange(IMG_DEV, dtype=jnp.int32)[None, :]
    shuffle = jnp.argsort(shuffle_key, axis=1)
    dest = jnp.take_along_axis(dest, shuffle, axis=1).reshape(-1).astype(jnp.int32)
    one_hot = (dest[:, None] == jnp.arange(REQS, dtype=jnp.int32)[None, :]).astype(jnp.int32)
    rank = jnp.sum((jnp.cumsum(one_hot, axis=0) - one_hot) * one_hot, axis=1)
    counts = jnp.sum(one_hot, axis=0)
    request_ids = jnp.arange(REQS, dtype=jnp.int32)
    longest = jnp.argmax(counts).astype(jnp.int32)
    others = jnp.where(request_ids == longest, -1, counts)
    second = jnp.argmax(others).astype(jnp.int32)
    offset = jax.random.randint(key_offset, (REQS,), 8, 64)
    offset = jnp.where(request_ids == longest, PROMPT - 16 - counts, jnp.where(request_ids == second, 8, offset)).astype(jnp.int32)
    position = (offset[dest] + rank).astype(jnp.int32)
    room = PROMPT - offset - counts
    tail = jax.random.randint(key_tail, (REQS,), 16, room + 1)
    lengths = jnp.where(request_ids == longest, PROMPT, offset + counts + tail).astype(jnp.int32)
    return (dest, position, lengths)


def draw_row_request(key, part):
    return layout(key)[0]


def draw_row_position(key, part):
    return layout(key)[1]


def draw_prompt_lengths(key, part):
    return layout(key)[2]


def draw_queries(key, part):
    own_key = jax.random.fold_in(key, 21)
    base = jnp.clip(jax.random.normal(own_key, (REQS, PROMPT, QH, HD), jnp.float32), -6.0, 6.0)
    return base.astype(jnp.bfloat16)


def draw_text_kv(key, part):
    own_key = jax.random.fold_in(key, 31)
    base = jnp.clip(jax.random.normal(own_key, (REQS, PROMPT, KVH, 2 * HD), jnp.float32), -6.0, 6.0)
    return base.astype(jnp.bfloat16)


def block_scale(key, shape, cuts, smallest, largest):
    factor_of, own = 1.0, jax.random.fold_in(key, 6)
    for dim, parts in cuts:
        steps = jnp.exp(jax.random.uniform(jax.random.fold_in(own, dim), (parts,), jnp.float32, smallest / len(cuts), largest / len(cuts)))
        factor_of = factor_of * jnp.repeat(steps, shape[dim] // parts).reshape([-1 if axis == dim else 1 for axis in range(len(shape))])
    return factor_of


def bell_draw(key, shape, scale, limit, cuts=(), kind=jnp.bfloat16):
    values = scale * jax.random.normal(key, shape, jnp.float32)
    if cuts:
        values = values * block_scale(key, shape, cuts, -0.22, 0.18)
    return jnp.clip(values, -limit, limit).astype(kind)


def setup_inputs(seed: int = 0) -> dict:
    key_of = jax.random.split(jax.random.key(seed), 8)
    queries = draw_queries(jax.random.fold_in(key_of[7], 71), 0)
    text_kv = draw_text_kv(jax.random.fold_in(key_of[7], 71), 0)
    image_rows = bell_draw(key_of[2], (IMG_ROWS, D), 1.0, 6.0, ((0, 64), (1, 4)))
    row_request = draw_row_request(jax.random.fold_in(key_of[7], 71), 0)
    row_position = draw_row_position(jax.random.fold_in(key_of[7], 71), 0)
    prompt_lengths = draw_prompt_lengths(jax.random.fold_in(key_of[7], 71), 0)
    kv_weight = bell_draw(key_of[6], (D, KVH, 2 * HD), D ** -0.5, 0.078125, ((0, 4),))
    return {"queries": queries, "text_kv": text_kv, "image_rows": image_rows, "row_request": row_request, "row_position": row_position, "prompt_lengths": prompt_lengths, "kv_weight": kv_weight}


def rotate_keys(summed, positions, head_dim):
    half = head_dim // 2
    freqs = jnp.exp(jnp.arange(half, dtype=jnp.float32) * (-2.0 * math.log(1000000.0) / head_dim))
    angles = positions.astype(jnp.float32)[:, None, None] * freqs[None, None, :]
    cosine = jnp.cos(angles)
    sine = jnp.sin(angles)
    first = summed[..., :half]
    second = summed[..., half:head_dim]
    rotated = jnp.concatenate([first * cosine - second * sine, second * cosine + first * sine, summed[..., head_dim:]], axis=-1)
    return rotated.astype(jnp.bfloat16)


def attend(args):
    query_rows, prompt_kv, length = args
    group = QH // KVH
    grouped = query_rows.reshape(PROMPT, KVH, group, HD).astype(jnp.float32)
    keys = prompt_kv[..., :HD].astype(jnp.float32)
    values = prompt_kv[..., HD:].astype(jnp.float32)
    scores = jnp.einsum("qhgd,khd->hgqk", grouped, keys) * (HD ** -0.5)
    index = jnp.arange(PROMPT, dtype=jnp.int32)
    allowed = (index[None, :] <= index[:, None]) & (index[None, :] < length)
    scores = jnp.where(allowed, scores, jnp.float32(-1e30))
    highest = jnp.max(scores, axis=-1, keepdims=True)
    expo = jnp.exp(scores - highest)
    weights = (expo / jnp.sum(expo, axis=-1, keepdims=True)).astype(jnp.bfloat16)
    result = jnp.einsum("hgqk,khd->qhgd", weights.astype(jnp.float32), values)
    result = jnp.where(index[:, None, None, None] < length, result, jnp.float32(0.0))
    return result.reshape(PROMPT, QH, HD).astype(jnp.bfloat16)


def reference(queries, text_kv, image_rows, row_request, row_position, prompt_lengths, kv_weight):
    summed = jnp.dot(image_rows, kv_weight.reshape(D, KVH * 2 * HD), preferred_element_type=jnp.float32)
    summed = summed.reshape(IMG_ROWS, KVH, 2 * HD)
    image_kv = rotate_keys(summed, row_position, HD)
    prompt_kv = text_kv.at[row_request, row_position].set(image_kv)
    return lax.map(attend, (queries, prompt_kv, prompt_lengths))
```

```python
import functools
import math

import jax
import jax.numpy as jnp
from jax import lax
from jax.experimental import pallas as pl
from jax.experimental.pallas import tpu as pltpu
from jax.sharding import PartitionSpec as P


def rotate_keys(summed, positions, head_dim):
    half = head_dim // 2
    freqs = jnp.exp(jnp.arange(half, dtype=jnp.float32) * (-2.0 * math.log(1000000.0) / head_dim))
    angles = positions.astype(jnp.float32)[:, None] * freqs[None, :]
    cosine = jnp.cos(angles)
    sine = jnp.sin(angles)
    first = summed[..., :half]
    second = summed[..., half:head_dim]
    rotated = jnp.concatenate(
        [first * cosine - second * sine, second * cosine + first * sine, summed[..., head_dim:]],
        axis=-1,
    )
    return rotated.astype(jnp.bfloat16)


def attention_kernel(block, head_dim, len_ref, q_ref, kv_ref, o_ref):
    prompt = q_ref.shape[1]
    length = len_ref[0]
    scale = head_dim ** (-0.5)
    for index in range(prompt // block):
        row_start = index * block
        keys_used = row_start + block
        query = q_ref[0, row_start:keys_used, :]
        keys = kv_ref[0:keys_used, 0:head_dim]
        scores = lax.dot_general(
            query, keys, (((1,), (1,)), ((), ())), preferred_element_type=jnp.float32
        ) * scale
        query_index = row_start + lax.broadcasted_iota(jnp.int32, (block, 1), 0)
        limit = jnp.minimum(query_index, length - 1)
        key_index = lax.broadcasted_iota(jnp.int32, (1, keys_used), 1)
        scores = jnp.where(key_index <= limit, scores, jnp.float32(-1e30))
        highest = jnp.max(scores, axis=-1, keepdims=True)
        expo = jnp.exp(scores - highest)
        total = jnp.sum(expo, axis=-1, keepdims=True)
        weights = (expo * (1.0 / total)).astype(jnp.bfloat16)
        values = kv_ref[0:keys_used, head_dim:]
        result = jnp.dot(weights, values, preferred_element_type=jnp.float32)
        result = jnp.where(query_index < length, result, jnp.float32(0.0))
        o_ref[0, row_start:keys_used, :] = result.astype(o_ref.dtype)


def attend(heads_first, prompt_kv, length, head_dim, block=256):
    heads, prompt, _ = heads_first.shape
    grid_spec = pltpu.PrefetchScalarGridSpec(
        num_scalar_prefetch=1,
        grid=(heads,),
        in_specs=[
            pl.BlockSpec((1, prompt, head_dim), lambda h, lens: (h, 0, 0)),
            pl.BlockSpec((prompt, 2 * head_dim), lambda h, lens: (0, 0)),
        ],
        out_specs=pl.BlockSpec((1, prompt, head_dim), lambda h, lens: (h, 0, 0)),
    )
    return pl.pallas_call(
        functools.partial(attention_kernel, block, head_dim),
        grid_spec=grid_spec,
        out_shape=jax.ShapeDtypeStruct((heads, prompt, head_dim), jnp.bfloat16),
        compiler_params=pltpu.CompilerParams(dimension_semantics=("arbitrary",)),
    )(length, heads_first, prompt_kv)


def per_device(queries, text_kv, image_rows, row_request, row_position, prompt_lengths, kv_weight):
    groups = lax.axis_size("req")
    own_rows = image_rows.shape[0]
    capacity = 2 * own_rows // groups
    prompt = queries.shape[1]
    head_dim = queries.shape[3]
    partial = jnp.einsum("rd,dhc->hrc", image_rows, kv_weight, preferred_element_type=jnp.float32)
    summed = lax.psum_scatter(partial, "tp", scatter_dimension=0, tiled=True)[0]
    image_kv = rotate_keys(summed, row_position, head_dim)
    one_hot = (row_request[:, None] == jnp.arange(groups, dtype=jnp.int32)[None, :]).astype(
        jnp.int32
    )
    before = jnp.cumsum(one_hot, axis=0) - one_hot
    slot_index = jnp.sum(before * one_hot, axis=1)
    target = row_request * capacity + slot_index
    pos_buffer = (
        jnp.full((groups * capacity,), prompt, jnp.int32)
        .at[target]
        .set(row_position)
        .reshape(groups, capacity)
    )
    kv_buffer = (
        jnp.zeros((groups * capacity, image_kv.shape[1]), jnp.bfloat16)
        .at[target]
        .set(image_kv)
        .reshape(groups, capacity, image_kv.shape[1])
    )
    got_kv = lax.all_to_all(kv_buffer, "req", split_axis=0, concat_axis=0, tiled=True)
    got_pos = lax.all_to_all(pos_buffer, "req", split_axis=0, concat_axis=0, tiled=True)
    places = got_pos.reshape(groups * capacity)
    flat_kv = got_kv.reshape(groups * capacity, image_kv.shape[1])
    prompt_kv = text_kv[0, :, 0, :].at[places].set(flat_kv, mode="drop")
    heads_first = jnp.transpose(queries[0], (1, 0, 2))
    out = attend(heads_first, prompt_kv, prompt_lengths, head_dim)
    return jnp.transpose(out, (1, 0, 2))[None]


def solution(mesh):
    in_specs = (
        P("req", None, "tp", None),
        P("req", None, "tp", None),
        P("req", "tp"),
        P("req"),
        P("req"),
        P("req"),
        P("tp", None, None),
    )
    out_specs = P("req", None, "tp", None)
    return jax.shard_map(
        per_device, mesh=mesh, in_specs=in_specs, out_specs=out_specs, check_vma=False
    )
```

```python
import functools
import math

import jax
import jax.numpy as jnp
from jax import lax
from jax.experimental import pallas as pl
from jax.experimental.pallas import tpu as pltpu
from jax.sharding import PartitionSpec as P


def rotate_keys(summed, positions, head_dim):
    half = head_dim // 2
    freqs = jnp.exp(jnp.arange(half, dtype=jnp.float32) * (-2.0 * math.log(1000000.0) / head_dim))
    angles = positions.astype(jnp.float32)[:, None] * freqs[None, :]
    cosine = jnp.cos(angles)
    sine = jnp.sin(angles)
    first = summed[..., :half]
    second = summed[..., half:head_dim]
    rotated = jnp.concatenate(
        [first * cosine - second * sine, second * cosine + first * sine, summed[..., head_dim:]],
        axis=-1,
    )
    return rotated.astype(jnp.bfloat16)


def attention_kernel(block, head_dim, len_ref, q_ref, kv_ref, o_ref):
    prompt = q_ref.shape[1]
    length = len_ref[0]
    scale = head_dim ** (-0.5)
    for index in range(prompt // block):
        row_start = index * block
        keys_used = row_start + block
        query = q_ref[0, row_start:keys_used, :]
        keys = kv_ref[0:keys_used, 0:head_dim]
        scores = lax.dot_general(
            query, keys, (((1,), (1,)), ((), ())), preferred_element_type=jnp.float32
        ) * scale
        query_index = row_start + lax.broadcasted_iota(jnp.int32, (block, 1), 0)
        limit = jnp.minimum(query_index, length - 1)
        key_index = lax.broadcasted_iota(jnp.int32, (1, keys_used), 1)
        scores = jnp.where(key_index <= limit, scores, jnp.float32(-1e30))
        highest = jnp.max(scores, axis=-1, keepdims=True)
        expo = jnp.exp(scores - highest)
        total = jnp.sum(expo, axis=-1, keepdims=True)
        weights = (expo * (1.0 / total)).astype(jnp.bfloat16)
        values = kv_ref[0:keys_used, head_dim:]
        result = jnp.dot(weights, values, preferred_element_type=jnp.float32)
        result = jnp.where(query_index < length, result, jnp.float32(0.0))
        o_ref[0, row_start:keys_used, :] = result.astype(o_ref.dtype)


def attend(heads_first, prompt_kv, length, head_dim, block=256):
    heads, prompt, _ = heads_first.shape
    grid_spec = pltpu.PrefetchScalarGridSpec(
        num_scalar_prefetch=1,
        grid=(heads,),
        in_specs=[
            pl.BlockSpec((1, prompt, head_dim), lambda h, lens: (h, 0, 0)),
            pl.BlockSpec((prompt, 2 * head_dim), lambda h, lens: (0, 0)),
        ],
        out_specs=pl.BlockSpec((1, prompt, head_dim), lambda h, lens: (h, 0, 0)),
    )
    return pl.pallas_call(
        functools.partial(attention_kernel, block, head_dim),
        grid_spec=grid_spec,
        out_shape=jax.ShapeDtypeStruct((heads, prompt, head_dim), jnp.bfloat16),
        compiler_params=pltpu.CompilerParams(dimension_semantics=("arbitrary",)),
    )(length, heads_first, prompt_kv)


def per_device(queries, text_kv, image_rows, row_request, row_position, prompt_lengths, kv_weight):
    groups = lax.axis_size("req")
    own_rows = image_rows.shape[0]
    capacity = 2 * own_rows // groups
    prompt = queries.shape[1]
    head_dim = queries.shape[3]
    width = 2 * head_dim
    partial = jnp.einsum("rd,dhc->hrc", image_rows, kv_weight, preferred_element_type=jnp.float32)
    summed = lax.psum_scatter(
        partial.astype(jnp.bfloat16), "tp", scatter_dimension=0, tiled=True
    )[0].astype(jnp.float32)
    image_kv = rotate_keys(summed, row_position, head_dim)
    one_hot = (row_request[:, None] == jnp.arange(groups, dtype=jnp.int32)[None, :]).astype(
        jnp.int32
    )
    before = jnp.cumsum(one_hot, axis=0) - one_hot
    slot_index = jnp.sum(before * one_hot, axis=1)
    target = row_request * capacity + slot_index
    slots = groups * capacity
    pick = (target[None, :] == jnp.arange(slots, dtype=jnp.int32)[:, None]).astype(jnp.bfloat16)
    send_kv = jnp.dot(pick, image_kv, preferred_element_type=jnp.float32).astype(jnp.bfloat16)
    pos_f = row_position.astype(jnp.float32)
    digits = jnp.stack([jnp.floor(pos_f / 16.0), pos_f - 16.0 * jnp.floor(pos_f / 16.0)], axis=1)
    send_pos = jnp.dot(pick.astype(jnp.float32), digits, precision=lax.Precision.HIGHEST)
    filled = jnp.sum(pick.astype(jnp.float32), axis=1, keepdims=True)
    send_pos = jnp.where(filled > 0, send_pos, jnp.float32(prompt / 16.0) * jnp.array([1.0, 0.0]))
    tail = send_pos.reshape(groups, 2 * capacity).astype(jnp.bfloat16)
    tail = jnp.pad(tail, ((0, 0), (0, 128 - 2 * capacity)))
    packet = jnp.concatenate([send_kv.reshape(groups, capacity * width), tail], axis=1)
    got = lax.all_to_all(packet, "req", split_axis=0, concat_axis=0, tiled=True)
    got_kv = got[:, : capacity * width].reshape(slots, width)
    got_digits = got[:, capacity * width : capacity * width + 2 * capacity].astype(jnp.int32)
    got_digits = got_digits.reshape(slots, 2)
    places = got_digits[:, 0] * 16 + got_digits[:, 1]
    place = (places[None, :] == jnp.arange(prompt, dtype=jnp.int32)[:, None]).astype(jnp.bfloat16)
    placed = jnp.dot(place, got_kv, preferred_element_type=jnp.float32).astype(jnp.bfloat16)
    hit = jnp.any(places[None, :] == jnp.arange(prompt, dtype=jnp.int32)[:, None], axis=1)
    prompt_kv = jnp.where(hit[:, None], placed, text_kv[0, :, 0, :])
    heads_first = jnp.transpose(queries[0], (1, 0, 2))
    out = attend(heads_first, prompt_kv, prompt_lengths, head_dim)
    return jnp.transpose(out, (1, 0, 2))[None]


def solution(mesh):
    in_specs = (
        P("req", None, "tp", None),
        P("req", None, "tp", None),
        P("req", "tp"),
        P("req"),
        P("req"),
        P("req"),
        P("tp", None, None),
    )
    out_specs = P("req", None, "tp", None)
    return jax.shard_map(
        per_device, mesh=mesh, in_specs=in_specs, out_specs=out_specs, check_vma=False
    )
```

```python
import functools
import math

import jax
import jax.numpy as jnp
from jax import lax
from jax.experimental import pallas as pl
from jax.experimental.pallas import tpu as pltpu
from jax.sharding import PartitionSpec as P


def rotate_keys(summed, positions, head_dim):
    half = head_dim // 2
    freqs = jnp.exp(jnp.arange(half, dtype=jnp.float32) * (-2.0 * math.log(1000000.0) / head_dim))
    angles = positions.astype(jnp.float32)[:, None] * freqs[None, :]
    cosine = jnp.cos(angles)
    sine = jnp.sin(angles)
    first = summed[..., :half]
    second = summed[..., half:head_dim]
    rotated = jnp.concatenate(
        [first * cosine - second * sine, second * cosine + first * sine, summed[..., head_dim:]],
        axis=-1,
    )
    return rotated.astype(jnp.bfloat16)


def attention_kernel(block, head_dim, len_ref, q_ref, kv_ref, o_ref):
    prompt = q_ref.shape[1]
    length = len_ref[0]
    scale = head_dim ** (-0.5)
    for index in range(prompt // block):
        row_start = index * block
        keys_used = row_start + block
        query = q_ref[0, row_start:keys_used, :]
        keys = kv_ref[0:keys_used, 0:head_dim]
        scores = lax.dot_general(
            query, keys, (((1,), (1,)), ((), ())), preferred_element_type=jnp.float32
        ) * scale
        query_index = row_start + lax.broadcasted_iota(jnp.int32, (block, 1), 0)
        limit = jnp.minimum(query_index, length - 1)
        key_index = lax.broadcasted_iota(jnp.int32, (1, keys_used), 1)
        scores = jnp.where(key_index <= limit, scores, jnp.float32(-1e30))
        highest = jnp.max(scores, axis=-1, keepdims=True)
        expo = jnp.exp(scores - highest)
        total = jnp.sum(expo, axis=-1, keepdims=True)
        weights = (expo * (1.0 / total)).astype(jnp.bfloat16)
        values = kv_ref[0:keys_used, head_dim:]
        result = jnp.dot(weights, values, preferred_element_type=jnp.float32)
        result = jnp.where(query_index < length, result, jnp.float32(0.0))
        o_ref[0, row_start:keys_used, :] = result.astype(o_ref.dtype)


def attend(heads_first, prompt_kv, length, head_dim, block=256):
    heads, prompt, _ = heads_first.shape
    grid_spec = pltpu.PrefetchScalarGridSpec(
        num_scalar_prefetch=1,
        grid=(heads,),
        in_specs=[
            pl.BlockSpec((1, prompt, head_dim), lambda h, lens: (h, 0, 0)),
            pl.BlockSpec((prompt, 2 * head_dim), lambda h, lens: (0, 0)),
        ],
        out_specs=pl.BlockSpec((1, prompt, head_dim), lambda h, lens: (h, 0, 0)),
    )
    return pl.pallas_call(
        functools.partial(attention_kernel, block, head_dim),
        grid_spec=grid_spec,
        out_shape=jax.ShapeDtypeStruct((heads, prompt, head_dim), jnp.bfloat16),
        compiler_params=pltpu.CompilerParams(dimension_semantics=("arbitrary",)),
    )(length, heads_first, prompt_kv)


def per_device(queries, text_kv, image_rows, row_request, row_position, prompt_lengths, kv_weight):
    groups = lax.axis_size("req")
    own_rows = image_rows.shape[0]
    capacity = 2 * own_rows // groups
    prompt = queries.shape[1]
    head_dim = queries.shape[3]
    width = 2 * head_dim
    partial = jnp.einsum("rd,dhc->hrc", image_rows, kv_weight, preferred_element_type=jnp.float32)
    summed = jnp.sum(lax.all_to_all(partial, "tp", split_axis=0, concat_axis=0, tiled=True), axis=0)
    image_kv = rotate_keys(summed, row_position, head_dim)
    one_hot = (row_request[:, None] == jnp.arange(groups, dtype=jnp.int32)[None, :]).astype(
        jnp.int32
    )
    before = jnp.cumsum(one_hot, axis=0) - one_hot
    slot_index = jnp.sum(before * one_hot, axis=1)
    target = row_request * capacity + slot_index
    slots = groups * capacity
    pick = (target[None, :] == jnp.arange(slots, dtype=jnp.int32)[:, None]).astype(jnp.bfloat16)
    send_kv = jnp.dot(pick, image_kv, preferred_element_type=jnp.float32).astype(jnp.bfloat16)
    pos_f = row_position.astype(jnp.float32)
    digits = jnp.stack([jnp.floor(pos_f / 16.0), pos_f - 16.0 * jnp.floor(pos_f / 16.0)], axis=1)
    send_pos = jnp.dot(pick.astype(jnp.float32), digits, precision=lax.Precision.HIGHEST)
    filled = jnp.sum(pick.astype(jnp.float32), axis=1, keepdims=True)
    send_pos = jnp.where(filled > 0, send_pos, jnp.float32(prompt / 16.0) * jnp.array([1.0, 0.0]))
    tail = send_pos.reshape(groups, 2 * capacity).astype(jnp.bfloat16)
    tail = jnp.pad(tail, ((0, 0), (0, 128 - 2 * capacity)))
    packet = jnp.concatenate([send_kv.reshape(groups, capacity * width), tail], axis=1)
    got = lax.all_to_all(packet, "req", split_axis=0, concat_axis=0, tiled=True)
    got_kv = got[:, : capacity * width].reshape(slots, width)
    got_digits = got[:, capacity * width : capacity * width + 2 * capacity].astype(jnp.int32)
    got_digits = got_digits.reshape(slots, 2)
    places = got_digits[:, 0] * 16 + got_digits[:, 1]
    place = (places[None, :] == jnp.arange(prompt, dtype=jnp.int32)[:, None]).astype(jnp.bfloat16)
    placed = jnp.dot(place, got_kv, preferred_element_type=jnp.float32).astype(jnp.bfloat16)
    hit = jnp.any(places[None, :] == jnp.arange(prompt, dtype=jnp.int32)[:, None], axis=1)
    prompt_kv = jnp.where(hit[:, None], placed, text_kv[0, :, 0, :])
    heads_first = jnp.transpose(queries[0], (1, 0, 2))
    out = attend(heads_first, prompt_kv, prompt_lengths, head_dim)
    return jnp.transpose(out, (1, 0, 2))[None]


def solution(mesh):
    in_specs = (
        P("req", None, "tp", None),
        P("req", None, "tp", None),
        P("req", "tp"),
        P("req"),
        P("req"),
        P("req"),
        P("tp", None, None),
    )
    out_specs = P("req", None, "tp", None)
    return jax.shard_map(
        per_device, mesh=mesh, in_specs=in_specs, out_specs=out_specs, check_vma=False
    )
```

```python
import functools
import math

import jax
import jax.numpy as jnp
from jax import lax
from jax.experimental import pallas as pl
from jax.experimental.pallas import tpu as pltpu
from jax.sharding import PartitionSpec as P


def rotate_keys(summed, positions, head_dim):
    half = head_dim // 2
    freqs = jnp.exp(jnp.arange(half, dtype=jnp.float32) * (-2.0 * math.log(1000000.0) / head_dim))
    angles = positions.astype(jnp.float32)[:, None] * freqs[None, :]
    cosine = jnp.cos(angles)
    sine = jnp.sin(angles)
    first = summed[..., :half]
    second = summed[..., half:head_dim]
    rotated = jnp.concatenate(
        [first * cosine - second * sine, second * cosine + first * sine, summed[..., head_dim:]],
        axis=-1,
    )
    return rotated.astype(jnp.bfloat16)


def attention_kernel(block, head_dim, len_ref, q_ref, kv_ref, o_ref):
    prompt = q_ref.shape[1]
    length = len_ref[0]
    scale = head_dim ** (-0.5)
    contract = (((1,), (1,)), ((), ()))
    for index in range(prompt // block):
        row_start = index * block
        keys_used = row_start + block

        @pl.when(row_start < length)
        def _():
            query = q_ref[0, row_start:keys_used, :]
            diag = lax.dot_general(
                query, kv_ref[row_start:keys_used, 0:head_dim], contract,
                preferred_element_type=jnp.float32,
            ) * scale
            query_index = row_start + lax.broadcasted_iota(jnp.int32, (block, 1), 0)
            limit = jnp.minimum(query_index, length - 1)
            key_index = row_start + lax.broadcasted_iota(jnp.int32, (1, block), 1)
            diag = jnp.where(key_index <= limit, diag, jnp.float32(-1e30))
            highest = jnp.max(diag, axis=-1, keepdims=True)
            if row_start:
                off = lax.dot_general(
                    query, kv_ref[0:row_start, 0:head_dim], contract,
                    preferred_element_type=jnp.float32,
                ) * scale
                highest = jnp.maximum(highest, jnp.max(off, axis=-1, keepdims=True))
            expo_diag = jnp.exp(diag - highest)
            total = jnp.sum(expo_diag, axis=-1, keepdims=True)
            if row_start:
                expo_off = jnp.exp(off - highest)
                total = total + jnp.sum(expo_off, axis=-1, keepdims=True)
            inverse = 1.0 / total
            result = jnp.dot(
                (expo_diag * inverse).astype(jnp.bfloat16),
                kv_ref[row_start:keys_used, head_dim:],
                preferred_element_type=jnp.float32,
            )
            if row_start:
                result = result + jnp.dot(
                    (expo_off * inverse).astype(jnp.bfloat16),
                    kv_ref[0:row_start, head_dim:],
                    preferred_element_type=jnp.float32,
                )
            result = jnp.where(query_index < length, result, jnp.float32(0.0))
            o_ref[0, row_start:keys_used, :] = result.astype(o_ref.dtype)

        @pl.when(row_start >= length)
        def _():
            o_ref[0, row_start:keys_used, :] = jnp.zeros((block, head_dim), o_ref.dtype)


def attend(heads_first, prompt_kv, length, head_dim, block=256):
    heads, prompt, _ = heads_first.shape
    grid_spec = pltpu.PrefetchScalarGridSpec(
        num_scalar_prefetch=1,
        grid=(heads,),
        in_specs=[
            pl.BlockSpec((1, prompt, head_dim), lambda h, lens: (h, 0, 0)),
            pl.BlockSpec((prompt, 2 * head_dim), lambda h, lens: (0, 0)),
        ],
        out_specs=pl.BlockSpec((1, prompt, head_dim), lambda h, lens: (h, 0, 0)),
    )
    return pl.pallas_call(
        functools.partial(attention_kernel, block, head_dim),
        grid_spec=grid_spec,
        out_shape=jax.ShapeDtypeStruct((heads, prompt, head_dim), jnp.bfloat16),
        compiler_params=pltpu.CompilerParams(dimension_semantics=("arbitrary",)),
    )(length, heads_first, prompt_kv)


def per_device(queries, text_kv, image_rows, row_request, row_position, prompt_lengths, kv_weight):
    groups = lax.axis_size("req")
    own_rows = image_rows.shape[0]
    capacity = 2 * own_rows // groups
    prompt = queries.shape[1]
    head_dim = queries.shape[3]
    width = 2 * head_dim
    partial = jnp.einsum("rd,dhc->hrc", image_rows, kv_weight, preferred_element_type=jnp.float32)
    summed = jnp.sum(lax.all_to_all(partial, "tp", split_axis=0, concat_axis=0, tiled=True), axis=0)
    image_kv = rotate_keys(summed, row_position, head_dim)
    one_hot = (row_request[:, None] == jnp.arange(groups, dtype=jnp.int32)[None, :]).astype(
        jnp.int32
    )
    before = jnp.cumsum(one_hot, axis=0) - one_hot
    slot_index = jnp.sum(before * one_hot, axis=1)
    target = row_request * capacity + slot_index
    slots = groups * capacity
    pick = (target[None, :] == jnp.arange(slots, dtype=jnp.int32)[:, None]).astype(jnp.bfloat16)
    send_kv = jnp.dot(pick, image_kv, preferred_element_type=jnp.float32).astype(jnp.bfloat16)
    pos_f = row_position.astype(jnp.float32)
    digits = jnp.stack([jnp.floor(pos_f / 16.0), pos_f - 16.0 * jnp.floor(pos_f / 16.0)], axis=1)
    send_pos = jnp.dot(pick.astype(jnp.float32), digits, precision=lax.Precision.HIGHEST)
    filled = jnp.sum(pick.astype(jnp.float32), axis=1, keepdims=True)
    send_pos = jnp.where(filled > 0, send_pos, jnp.float32(prompt / 16.0) * jnp.array([1.0, 0.0]))
    tail = send_pos.reshape(groups, 2 * capacity).astype(jnp.bfloat16)
    tail = jnp.pad(tail, ((0, 0), (0, 128 - 2 * capacity)))
    packet = jnp.concatenate([send_kv.reshape(groups, capacity * width), tail], axis=1)
    got = lax.all_to_all(packet, "req", split_axis=0, concat_axis=0, tiled=True)
    got_kv = got[:, : capacity * width].reshape(slots, width)
    got_digits = got[:, capacity * width : capacity * width + 2 * capacity].astype(jnp.int32)
    got_digits = got_digits.reshape(slots, 2)
    places = got_digits[:, 0] * 16 + got_digits[:, 1]
    place = (places[None, :] == jnp.arange(prompt, dtype=jnp.int32)[:, None]).astype(jnp.bfloat16)
    placed = jnp.dot(place, got_kv, preferred_element_type=jnp.float32).astype(jnp.bfloat16)
    hit = jnp.any(places[None, :] == jnp.arange(prompt, dtype=jnp.int32)[:, None], axis=1)
    prompt_kv = jnp.where(hit[:, None], placed, text_kv[0, :, 0, :])
    heads_first = jnp.transpose(queries[0], (1, 0, 2))
    out = attend(heads_first, prompt_kv, prompt_lengths, head_dim)
    return jnp.transpose(out, (1, 0, 2))[None]


def solution(mesh):
    in_specs = (
        P("req", None, "tp", None),
        P("req", None, "tp", None),
        P("req", "tp"),
        P("req"),
        P("req"),
        P("req"),
        P("tp", None, None),
    )
    out_specs = P("req", None, "tp", None)
    return jax.shard_map(
        per_device, mesh=mesh, in_specs=in_specs, out_specs=out_specs, check_vma=False
    )
```

```python
import functools
import math

import jax
import jax.numpy as jnp
from jax import lax
from jax.experimental import pallas as pl
from jax.experimental.pallas import tpu as pltpu
from jax.sharding import PartitionSpec as P


def rotate_keys(summed, positions, head_dim):
    half = head_dim // 2
    freqs = jnp.exp(jnp.arange(half, dtype=jnp.float32) * (-2.0 * math.log(1000000.0) / head_dim))
    angles = positions.astype(jnp.float32)[:, None] * freqs[None, :]
    cosine = jnp.cos(angles)
    sine = jnp.sin(angles)
    first = summed[..., :half]
    second = summed[..., half:head_dim]
    rotated = jnp.concatenate(
        [first * cosine - second * sine, second * cosine + first * sine, summed[..., head_dim:]],
        axis=-1,
    )
    return rotated.astype(jnp.bfloat16)


def attention_kernel(block, head_dim, len_ref, q_ref, kv_ref, o_ref):
    prompt = q_ref.shape[1]
    length = len_ref[0]
    scale = head_dim ** (-0.5)
    for index in range(prompt // block):
        row_start = index * block
        keys_used = row_start + block
        query = q_ref[0, row_start:keys_used, :]
        keys = kv_ref[0:keys_used, 0:head_dim]
        scores = lax.dot_general(
            query, keys, (((1,), (1,)), ((), ())), preferred_element_type=jnp.float32
        ) * scale
        query_index = row_start + lax.broadcasted_iota(jnp.int32, (block, 1), 0)
        limit = jnp.minimum(query_index, length - 1)
        key_index = lax.broadcasted_iota(jnp.int32, (1, keys_used), 1)
        scores = jnp.where(key_index <= limit, scores, jnp.float32(-1e30))
        highest = jnp.max(scores, axis=-1, keepdims=True)
        expo = jnp.exp(scores - highest)
        total = jnp.sum(expo, axis=-1, keepdims=True)
        weights = (expo * (1.0 / total)).astype(jnp.bfloat16)
        values = kv_ref[0:keys_used, head_dim:]
        result = jnp.dot(weights, values, preferred_element_type=jnp.float32)
        result = jnp.where(query_index < length, result, jnp.float32(0.0))
        o_ref[0, row_start:keys_used, :] = result.astype(o_ref.dtype)


def attend(heads_first, prompt_kv, length, head_dim, block=256):
    heads, prompt, _ = heads_first.shape
    grid_spec = pltpu.PrefetchScalarGridSpec(
        num_scalar_prefetch=1,
        grid=(heads,),
        in_specs=[
            pl.BlockSpec((1, prompt, head_dim), lambda h, lens: (h, 0, 0)),
            pl.BlockSpec((prompt, 2 * head_dim), lambda h, lens: (0, 0)),
        ],
        out_specs=pl.BlockSpec((1, prompt, head_dim), lambda h, lens: (h, 0, 0)),
    )
    return pl.pallas_call(
        functools.partial(attention_kernel, block, head_dim),
        grid_spec=grid_spec,
        out_shape=jax.ShapeDtypeStruct((heads, prompt, head_dim), jnp.bfloat16),
        compiler_params=pltpu.CompilerParams(dimension_semantics=("arbitrary",)),
    )(length, heads_first, prompt_kv)


def per_device(queries, text_kv, image_rows, row_request, row_position, prompt_lengths, kv_weight):
    groups = lax.axis_size("req")
    own_rows = image_rows.shape[0]
    capacity = 2 * own_rows // groups
    prompt = queries.shape[1]
    head_dim = queries.shape[3]
    width = 2 * head_dim
    partial = jnp.einsum("rd,dhc->hrc", image_rows, kv_weight, preferred_element_type=jnp.float32)
    me = lax.axis_index("tp")
    got = lax.all_to_all(partial.astype(jnp.bfloat16), "tp", split_axis=0, concat_axis=0, tiled=True)
    others = jnp.arange(partial.shape[0], dtype=jnp.int32)[:, None, None] != me
    own = lax.dynamic_index_in_dim(partial, me, axis=0, keepdims=False)
    summed = jnp.sum(jnp.where(others, got.astype(jnp.float32), 0.0), axis=0) + own
    image_kv = rotate_keys(summed, row_position, head_dim)
    one_hot = (row_request[:, None] == jnp.arange(groups, dtype=jnp.int32)[None, :]).astype(
        jnp.int32
    )
    before = jnp.cumsum(one_hot, axis=0) - one_hot
    slot_index = jnp.sum(before * one_hot, axis=1)
    target = row_request * capacity + slot_index
    slots = groups * capacity
    pick = (target[None, :] == jnp.arange(slots, dtype=jnp.int32)[:, None]).astype(jnp.bfloat16)
    send_kv = jnp.dot(pick, image_kv, preferred_element_type=jnp.float32).astype(jnp.bfloat16)
    pos_f = row_position.astype(jnp.float32)
    digits = jnp.stack([jnp.floor(pos_f / 16.0), pos_f - 16.0 * jnp.floor(pos_f / 16.0)], axis=1)
    send_pos = jnp.dot(pick.astype(jnp.float32), digits, precision=lax.Precision.HIGHEST)
    filled = jnp.sum(pick.astype(jnp.float32), axis=1, keepdims=True)
    send_pos = jnp.where(filled > 0, send_pos, jnp.float32(prompt / 16.0) * jnp.array([1.0, 0.0]))
    tail = send_pos.reshape(groups, 2 * capacity).astype(jnp.bfloat16)
    tail = jnp.pad(tail, ((0, 0), (0, 128 - 2 * capacity)))
    packet = jnp.concatenate([send_kv.reshape(groups, capacity * width), tail], axis=1)
    got = lax.all_to_all(packet, "req", split_axis=0, concat_axis=0, tiled=True)
    got_kv = got[:, : capacity * width].reshape(slots, width)
    got_digits = got[:, capacity * width : capacity * width + 2 * capacity].astype(jnp.int32)
    got_digits = got_digits.reshape(slots, 2)
    places = got_digits[:, 0] * 16 + got_digits[:, 1]
    place = (places[None, :] == jnp.arange(prompt, dtype=jnp.int32)[:, None]).astype(jnp.bfloat16)
    placed = jnp.dot(place, got_kv, preferred_element_type=jnp.float32).astype(jnp.bfloat16)
    hit = jnp.any(places[None, :] == jnp.arange(prompt, dtype=jnp.int32)[:, None], axis=1)
    prompt_kv = jnp.where(hit[:, None], placed, text_kv[0, :, 0, :])
    heads_first = jnp.transpose(queries[0], (1, 0, 2))
    out = attend(heads_first, prompt_kv, prompt_lengths, head_dim)
    return jnp.transpose(out, (1, 0, 2))[None]


def solution(mesh):
    in_specs = (
        P("req", None, "tp", None),
        P("req", None, "tp", None),
        P("req", "tp"),
        P("req"),
        P("req"),
        P("req"),
        P("tp", None, None),
    )
    out_specs = P("req", None, "tp", None)
    return jax.shard_map(
        per_device, mesh=mesh, in_specs=in_specs, out_specs=out_specs, check_vma=False
    )
```

```python
import functools
import math

import jax
import jax.numpy as jnp
from jax import lax
from jax.experimental import pallas as pl
from jax.experimental.pallas import tpu as pltpu
from jax.sharding import PartitionSpec as P


def rotate_keys(summed, positions, head_dim):
    half = head_dim // 2
    freqs = jnp.exp(jnp.arange(half, dtype=jnp.float32) * (-2.0 * math.log(1000000.0) / head_dim))
    angles = positions.astype(jnp.float32)[:, None] * freqs[None, :]
    cosine = jnp.cos(angles)
    sine = jnp.sin(angles)
    first = summed[..., :half]
    second = summed[..., half:head_dim]
    rotated = jnp.concatenate(
        [first * cosine - second * sine, second * cosine + first * sine, summed[..., head_dim:]],
        axis=-1,
    )
    return rotated.astype(jnp.bfloat16)


def attention_kernel(block, head_dim, len_ref, q_ref, kt_ref, vx_ref, o_ref):
    prompt = q_ref.shape[1]
    length = len_ref[0]
    scale = head_dim ** (-0.5)
    for index in range(prompt // block):
        row_start = index * block
        keys_used = row_start + block
        query = q_ref[0, row_start:keys_used, :]
        scores = jnp.dot(query, kt_ref[:, 0:keys_used], preferred_element_type=jnp.float32)
        query_index = row_start + lax.broadcasted_iota(jnp.int32, (block, 1), 0)
        limit = jnp.minimum(query_index, length - 1)
        key_index = lax.broadcasted_iota(jnp.int32, (1, keys_used), 1)
        scores = jnp.where(key_index <= limit, scores, jnp.float32(-1e30))
        highest = jnp.max(scores, axis=-1, keepdims=True)
        weights = jnp.exp((scores - highest) * scale).astype(jnp.bfloat16)
        both = jnp.dot(weights, vx_ref[0:keys_used, :], preferred_element_type=jnp.float32)
        result = both[:, :head_dim] / both[:, head_dim : head_dim + 1]
        result = jnp.where(query_index < length, result, jnp.float32(0.0))
        o_ref[0, row_start:keys_used, :] = result.astype(o_ref.dtype)


def attend(heads_first, prompt_kv, length, head_dim, block=256):
    heads, prompt, _ = heads_first.shape
    keys_t = jnp.transpose(prompt_kv[:, :head_dim])
    values_ext = jnp.concatenate(
        [prompt_kv[:, head_dim:], jnp.ones((prompt, head_dim), prompt_kv.dtype)], axis=1
    )
    grid_spec = pltpu.PrefetchScalarGridSpec(
        num_scalar_prefetch=1,
        grid=(heads,),
        in_specs=[
            pl.BlockSpec((1, prompt, head_dim), lambda h, lens: (h, 0, 0)),
            pl.BlockSpec((head_dim, prompt), lambda h, lens: (0, 0)),
            pl.BlockSpec((prompt, 2 * head_dim), lambda h, lens: (0, 0)),
        ],
        out_specs=pl.BlockSpec((1, prompt, head_dim), lambda h, lens: (h, 0, 0)),
    )
    return pl.pallas_call(
        functools.partial(attention_kernel, block, head_dim),
        grid_spec=grid_spec,
        out_shape=jax.ShapeDtypeStruct((heads, prompt, head_dim), jnp.bfloat16),
        compiler_params=pltpu.CompilerParams(dimension_semantics=("arbitrary",)),
    )(length, heads_first, keys_t, values_ext)


def per_device(queries, text_kv, image_rows, row_request, row_position, prompt_lengths, kv_weight):
    groups = lax.axis_size("req")
    own_rows = image_rows.shape[0]
    capacity = 2 * own_rows // groups
    prompt = queries.shape[1]
    head_dim = queries.shape[3]
    width = 2 * head_dim
    partial = jnp.einsum("rd,dhc->hrc", image_rows, kv_weight, preferred_element_type=jnp.float32)
    me = lax.axis_index("tp")
    got = lax.all_to_all(partial.astype(jnp.bfloat16), "tp", split_axis=0, concat_axis=0, tiled=True)
    others = jnp.arange(partial.shape[0], dtype=jnp.int32)[:, None, None] != me
    own = lax.dynamic_index_in_dim(partial, me, axis=0, keepdims=False)
    summed = jnp.sum(jnp.where(others, got.astype(jnp.float32), 0.0), axis=0) + own
    image_kv = rotate_keys(summed, row_position, head_dim)
    one_hot = (row_request[:, None] == jnp.arange(groups, dtype=jnp.int32)[None, :]).astype(
        jnp.int32
    )
    before = jnp.cumsum(one_hot, axis=0) - one_hot
    slot_index = jnp.sum(before * one_hot, axis=1)
    target = row_request * capacity + slot_index
    slots = groups * capacity
    pick = (target[None, :] == jnp.arange(slots, dtype=jnp.int32)[:, None]).astype(jnp.bfloat16)
    send_kv = jnp.dot(pick, image_kv, preferred_element_type=jnp.float32).astype(jnp.bfloat16)
    pos_f = row_position.astype(jnp.float32)
    digits = jnp.stack([jnp.floor(pos_f / 16.0), pos_f - 16.0 * jnp.floor(pos_f / 16.0)], axis=1)
    send_pos = jnp.dot(pick.astype(jnp.float32), digits, precision=lax.Precision.HIGHEST)
    filled = jnp.sum(pick.astype(jnp.float32), axis=1, keepdims=True)
    send_pos = jnp.where(filled > 0, send_pos, jnp.float32(prompt / 16.0) * jnp.array([1.0, 0.0]))
    tail = send_pos.reshape(groups, 2 * capacity).astype(jnp.bfloat16)
    tail = jnp.pad(tail, ((0, 0), (0, 128 - 2 * capacity)))
    packet = jnp.concatenate([send_kv.reshape(groups, capacity * width), tail], axis=1)
    got = lax.all_to_all(packet, "req", split_axis=0, concat_axis=0, tiled=True)
    got_kv = got[:, : capacity * width].reshape(slots, width)
    got_digits = got[:, capacity * width : capacity * width + 2 * capacity].astype(jnp.int32)
    got_digits = got_digits.reshape(slots, 2)
    places = got_digits[:, 0] * 16 + got_digits[:, 1]
    place = (places[None, :] == jnp.arange(prompt, dtype=jnp.int32)[:, None]).astype(jnp.bfloat16)
    placed = jnp.dot(place, got_kv, preferred_element_type=jnp.float32).astype(jnp.bfloat16)
    hit = jnp.any(places[None, :] == jnp.arange(prompt, dtype=jnp.int32)[:, None], axis=1)
    prompt_kv = jnp.where(hit[:, None], placed, text_kv[0, :, 0, :])
    heads_first = jnp.transpose(queries[0], (1, 0, 2))
    out = attend(heads_first, prompt_kv, prompt_lengths, head_dim)
    return jnp.transpose(out, (1, 0, 2))[None]


def solution(mesh):
    in_specs = (
        P("req", None, "tp", None),
        P("req", None, "tp", None),
        P("req", "tp"),
        P("req"),
        P("req"),
        P("req"),
        P("tp", None, None),
    )
    out_specs = P("req", None, "tp", None)
    return jax.shard_map(
        per_device, mesh=mesh, in_specs=in_specs, out_specs=out_specs, check_vma=False
    )
```

```python
import functools
import math

import jax
import jax.numpy as jnp
from jax import lax
from jax.experimental import pallas as pl
from jax.experimental.pallas import tpu as pltpu
from jax.sharding import PartitionSpec as P


def rotate_keys(summed, positions, head_dim):
    half = head_dim // 2
    freqs = jnp.exp(jnp.arange(half, dtype=jnp.float32) * (-2.0 * math.log(1000000.0) / head_dim))
    angles = positions.astype(jnp.float32)[:, None] * freqs[None, :]
    cosine = jnp.cos(angles)
    sine = jnp.sin(angles)
    first = summed[..., :half]
    second = summed[..., half:head_dim]
    rotated = jnp.concatenate(
        [first * cosine - second * sine, second * cosine + first * sine, summed[..., head_dim:]],
        axis=-1,
    )
    return rotated.astype(jnp.bfloat16)


def attention_kernel(block, head_dim, len_ref, q_ref, kt_ref, vx_ref, o_ref):
    prompt = q_ref.shape[1]
    length = len_ref[0]
    scale = head_dim ** (-0.5)
    for index in range(prompt // block):
        row_start = index * block
        keys_used = row_start + block
        query = q_ref[0, row_start:keys_used, :]
        scores = jnp.dot(query, kt_ref[:, 0:keys_used], preferred_element_type=jnp.float32)
        query_index = row_start + lax.broadcasted_iota(jnp.int32, (block, 1), 0)
        limit = jnp.minimum(query_index, length - 1)
        key_index = lax.broadcasted_iota(jnp.int32, (1, keys_used), 1)
        scores = jnp.where(key_index <= limit, scores, jnp.float32(-1e30))
        highest = jnp.max(scores, axis=-1, keepdims=True)
        weights = jnp.exp((scores - highest) * scale).astype(jnp.bfloat16)
        both = jnp.dot(weights, vx_ref[0:keys_used, :], preferred_element_type=jnp.float32)
        result = both[:, :head_dim] / both[:, head_dim : head_dim + 1]
        result = jnp.where(query_index < length, result, jnp.float32(0.0))
        o_ref[0, row_start:keys_used, :] = result.astype(o_ref.dtype)


def attend(heads_first, keys_t, values_ext, length, head_dim, block=256):
    heads, prompt, _ = heads_first.shape
    grid_spec = pltpu.PrefetchScalarGridSpec(
        num_scalar_prefetch=1,
        grid=(heads,),
        in_specs=[
            pl.BlockSpec((1, prompt, head_dim), lambda h, lens: (h, 0, 0)),
            pl.BlockSpec((head_dim, prompt), lambda h, lens: (0, 0)),
            pl.BlockSpec((prompt, 2 * head_dim), lambda h, lens: (0, 0)),
        ],
        out_specs=pl.BlockSpec((1, prompt, head_dim), lambda h, lens: (h, 0, 0)),
    )
    return pl.pallas_call(
        functools.partial(attention_kernel, block, head_dim),
        grid_spec=grid_spec,
        out_shape=jax.ShapeDtypeStruct((heads, prompt, head_dim), jnp.bfloat16),
        compiler_params=pltpu.CompilerParams(dimension_semantics=("arbitrary",)),
    )(length, heads_first, keys_t, values_ext)


def per_device(queries, text_kv, image_rows, row_request, row_position, prompt_lengths, kv_weight):
    groups = lax.axis_size("req")
    own_rows = image_rows.shape[0]
    capacity = 2 * own_rows // groups
    prompt = queries.shape[1]
    head_dim = queries.shape[3]
    width = 2 * head_dim
    me = lax.axis_index("tp")
    partial = jnp.einsum("rd,dhc->hrc", image_rows, kv_weight, preferred_element_type=jnp.bfloat16)
    got = lax.all_to_all(partial, "tp", split_axis=0, concat_axis=0, tiled=True)
    own_weight = lax.dynamic_index_in_dim(kv_weight, me, axis=1, keepdims=False)
    own = jnp.dot(image_rows, own_weight, preferred_element_type=jnp.float32)
    others = jnp.arange(partial.shape[0], dtype=jnp.int32)[:, None, None] != me
    summed = jnp.sum(jnp.where(others, got.astype(jnp.float32), 0.0), axis=0) + own
    image_kv = rotate_keys(summed, row_position, head_dim)
    one_hot = (row_request[:, None] == jnp.arange(groups, dtype=jnp.int32)[None, :]).astype(
        jnp.int32
    )
    before = jnp.cumsum(one_hot, axis=0) - one_hot
    slot_index = jnp.sum(before * one_hot, axis=1)
    target = row_request * capacity + slot_index
    slots = groups * capacity
    pick = (target[None, :] == jnp.arange(slots, dtype=jnp.int32)[:, None]).astype(jnp.bfloat16)
    send_kv = jnp.dot(pick, image_kv, preferred_element_type=jnp.float32).astype(jnp.bfloat16)
    pos_f = row_position.astype(jnp.float32) + 1.0
    digits = jnp.stack([jnp.floor(pos_f / 16.0), pos_f - 16.0 * jnp.floor(pos_f / 16.0)], axis=1)
    send_pos = jnp.dot(pick.astype(jnp.float32), digits, precision=lax.Precision.HIGHEST)
    tail = send_pos.reshape(groups, 2 * capacity).astype(jnp.bfloat16)
    tail = jnp.pad(tail, ((0, 0), (0, 128 - 2 * capacity)))
    packet = jnp.concatenate([send_kv.reshape(groups, capacity * width), tail], axis=1)
    text = text_kv[0, :, 0, :]
    text_keys_t = jnp.transpose(text[:, :head_dim])
    ones = jnp.ones((prompt, head_dim), text.dtype)
    text_values_ext = jnp.concatenate([text[:, head_dim:], ones], axis=1)
    got = lax.all_to_all(packet, "req", split_axis=0, concat_axis=0, tiled=True)
    got_kv = got[:, : capacity * width].reshape(slots, width)
    got_digits = got[:, capacity * width : capacity * width + 2 * capacity].astype(jnp.int32)
    got_digits = got_digits.reshape(slots, 2)
    places = got_digits[:, 0] * 16 + got_digits[:, 1] - 1
    match = places[None, :] == jnp.arange(prompt, dtype=jnp.int32)[:, None]
    place = match.astype(jnp.bfloat16)
    hit = jnp.any(match, axis=1)
    image_keys_t = jnp.einsum(
        "sd,ps->dp", got_kv[:, :head_dim], place, preferred_element_type=jnp.float32
    ).astype(jnp.bfloat16)
    image_values = jnp.dot(place, got_kv[:, head_dim:], preferred_element_type=jnp.float32)
    keys_t = jnp.where(hit[None, :], image_keys_t, text_keys_t)
    values_ext = jnp.where(
        hit[:, None], jnp.concatenate([image_values.astype(jnp.bfloat16), ones], axis=1),
        text_values_ext,
    )
    heads_first = jnp.transpose(queries[0], (1, 0, 2))
    out = attend(heads_first, keys_t, values_ext, prompt_lengths, head_dim)
    return jnp.transpose(out, (1, 0, 2))[None]


def solution(mesh):
    in_specs = (
        P("req", None, "tp", None),
        P("req", None, "tp", None),
        P("req", "tp"),
        P("req"),
        P("req"),
        P("req"),
        P("tp", None, None),
    )
    out_specs = P("req", None, "tp", None)
    return jax.shard_map(
        per_device, mesh=mesh, in_specs=in_specs, out_specs=out_specs, check_vma=False
    )
```

```python
import functools
import math

import jax
import jax.numpy as jnp
from jax import lax
from jax.experimental import pallas as pl
from jax.experimental.pallas import tpu as pltpu
from jax.sharding import PartitionSpec as P


def rotate_keys(summed, positions, head_dim):
    half = head_dim // 2
    freqs = jnp.exp(jnp.arange(half, dtype=jnp.float32) * (-2.0 * math.log(1000000.0) / head_dim))
    angles = positions.astype(jnp.float32)[:, None] * freqs[None, :]
    cosine = jnp.cos(angles)
    sine = jnp.sin(angles)
    first = summed[..., :half]
    second = summed[..., half:head_dim]
    rotated = jnp.concatenate(
        [first * cosine - second * sine, second * cosine + first * sine, summed[..., head_dim:]],
        axis=-1,
    )
    return rotated.astype(jnp.bfloat16)


def attention_kernel(block, head_dim, len_ref, q_ref, kt_ref, vx_ref, o_ref):
    prompt = q_ref.shape[1]
    length = len_ref[0]
    scale = head_dim ** (-0.5)
    for index in range(prompt // block):
        row_start = index * block
        keys_used = row_start + block
        query = q_ref[0, row_start:keys_used, :]
        scores = jnp.dot(query, kt_ref[:, 0:keys_used], preferred_element_type=jnp.float32)
        query_index = row_start + lax.broadcasted_iota(jnp.int32, (block, 1), 0)
        limit = jnp.minimum(query_index, length - 1)
        key_index = row_start + lax.broadcasted_iota(jnp.int32, (1, block), 1)
        diag = jnp.where(key_index <= limit, scores[:, row_start:], jnp.float32(-1e30))
        scores = jnp.concatenate([scores[:, :row_start], diag], axis=1) if row_start else diag
        highest = jnp.max(scores, axis=-1, keepdims=True)
        weights = jnp.exp((scores - highest) * scale).astype(jnp.bfloat16)
        both = jnp.dot(weights, vx_ref[0:keys_used, :], preferred_element_type=jnp.float32)
        result = both[:, :head_dim] / both[:, head_dim : head_dim + 1]
        result = jnp.where(query_index < length, result, jnp.float32(0.0))
        o_ref[0, row_start:keys_used, :] = result.astype(o_ref.dtype)


def attend(heads_first, keys_t, values_ext, length, head_dim, block=256):
    heads, prompt, _ = heads_first.shape
    grid_spec = pltpu.PrefetchScalarGridSpec(
        num_scalar_prefetch=1,
        grid=(heads,),
        in_specs=[
            pl.BlockSpec((1, prompt, head_dim), lambda h, lens: (h, 0, 0)),
            pl.BlockSpec((head_dim, prompt), lambda h, lens: (0, 0)),
            pl.BlockSpec((prompt, 2 * head_dim), lambda h, lens: (0, 0)),
        ],
        out_specs=pl.BlockSpec((1, prompt, head_dim), lambda h, lens: (h, 0, 0)),
    )
    return pl.pallas_call(
        functools.partial(attention_kernel, block, head_dim),
        grid_spec=grid_spec,
        out_shape=jax.ShapeDtypeStruct((heads, prompt, head_dim), jnp.bfloat16),
        compiler_params=pltpu.CompilerParams(dimension_semantics=("arbitrary",)),
    )(length, heads_first, keys_t, values_ext)


def per_device(queries, text_kv, image_rows, row_request, row_position, prompt_lengths, kv_weight):
    groups = lax.axis_size("req")
    own_rows = image_rows.shape[0]
    capacity = 2 * own_rows // groups
    prompt = queries.shape[1]
    head_dim = queries.shape[3]
    width = 2 * head_dim
    me = lax.axis_index("tp")
    partial = jnp.einsum("rd,dhc->hrc", image_rows, kv_weight, preferred_element_type=jnp.bfloat16)
    got = lax.all_to_all(partial, "tp", split_axis=0, concat_axis=0, tiled=True)
    own_weight = lax.dynamic_index_in_dim(kv_weight, me, axis=1, keepdims=False)
    own = jnp.dot(image_rows, own_weight, preferred_element_type=jnp.float32)
    others = jnp.arange(partial.shape[0], dtype=jnp.int32)[:, None, None] != me
    summed = jnp.sum(jnp.where(others, got.astype(jnp.float32), 0.0), axis=0) + own
    image_kv = rotate_keys(summed, row_position, head_dim)
    one_hot = (row_request[:, None] == jnp.arange(groups, dtype=jnp.int32)[None, :]).astype(
        jnp.int32
    )
    before = jnp.cumsum(one_hot, axis=0) - one_hot
    slot_index = jnp.sum(before * one_hot, axis=1)
    target = row_request * capacity + slot_index
    slots = groups * capacity
    pick = (target[None, :] == jnp.arange(slots, dtype=jnp.int32)[:, None]).astype(jnp.bfloat16)
    send_kv = jnp.dot(pick, image_kv, preferred_element_type=jnp.float32).astype(jnp.bfloat16)
    pos_f = row_position.astype(jnp.float32) + 1.0
    digits = jnp.stack([jnp.floor(pos_f / 16.0), pos_f - 16.0 * jnp.floor(pos_f / 16.0)], axis=1)
    send_pos = jnp.dot(pick.astype(jnp.float32), digits, precision=lax.Precision.HIGHEST)
    tail = send_pos.reshape(groups, 2 * capacity).astype(jnp.bfloat16)
    tail = jnp.pad(tail, ((0, 0), (0, 128 - 2 * capacity)))
    packet = jnp.concatenate([send_kv.reshape(groups, capacity * width), tail], axis=1)
    text = text_kv[0, :, 0, :]
    text_keys_t = jnp.transpose(text[:, :head_dim])
    ones = jnp.ones((prompt, head_dim), text.dtype)
    text_values_ext = jnp.concatenate([text[:, head_dim:], ones], axis=1)
    got = lax.all_to_all(packet, "req", split_axis=0, concat_axis=0, tiled=True)
    got_kv = got[:, : capacity * width].reshape(slots, width)
    got_digits = got[:, capacity * width : capacity * width + 2 * capacity].astype(jnp.int32)
    got_digits = got_digits.reshape(slots, 2)
    places = got_digits[:, 0] * 16 + got_digits[:, 1] - 1
    match = places[None, :] == jnp.arange(prompt, dtype=jnp.int32)[:, None]
    place = match.astype(jnp.bfloat16)
    hit = jnp.any(match, axis=1)
    image_keys_t = jnp.einsum(
        "sd,ps->dp", got_kv[:, :head_dim], place, preferred_element_type=jnp.float32
    ).astype(jnp.bfloat16)
    image_values = jnp.dot(place, got_kv[:, head_dim:], preferred_element_type=jnp.float32)
    keys_t = jnp.where(hit[None, :], image_keys_t, text_keys_t)
    values_ext = jnp.where(
        hit[:, None], jnp.concatenate([image_values.astype(jnp.bfloat16), ones], axis=1),
        text_values_ext,
    )
    heads_first = jnp.transpose(queries[0], (1, 0, 2))
    out = attend(heads_first, keys_t, values_ext, prompt_lengths, head_dim)
    return jnp.transpose(out, (1, 0, 2))[None]


def solution(mesh):
    in_specs = (
        P("req", None, "tp", None),
        P("req", None, "tp", None),
        P("req", "tp"),
        P("req"),
        P("req"),
        P("req"),
        P("tp", None, None),
    )
    out_specs = P("req", None, "tp", None)
    return jax.shard_map(
        per_device, mesh=mesh, in_specs=in_specs, out_specs=out_specs, check_vma=False
    )
```

```python
import functools
import math

import jax
import jax.numpy as jnp
from jax import lax
from jax.experimental import pallas as pl
from jax.experimental.pallas import tpu as pltpu
from jax.sharding import PartitionSpec as P


def rotate_keys(summed, positions, head_dim):
    half = head_dim // 2
    freqs = jnp.exp(jnp.arange(half, dtype=jnp.float32) * (-2.0 * math.log(1000000.0) / head_dim))
    angles = positions.astype(jnp.float32)[:, None] * freqs[None, :]
    cosine = jnp.cos(angles)
    sine = jnp.sin(angles)
    first = summed[..., :half]
    second = summed[..., half:head_dim]
    rotated = jnp.concatenate(
        [first * cosine - second * sine, second * cosine + first * sine, summed[..., head_dim:]],
        axis=-1,
    )
    return rotated.astype(jnp.bfloat16)


def attention_kernel(block, head_dim, len_ref, q_ref, kt_ref, vx_ref, o_ref):
    prompt = q_ref.shape[1]
    length = len_ref[0]
    scale = head_dim ** (-0.5)
    for index in range(prompt // block):
        row_start = index * block
        keys_used = row_start + block
        query = q_ref[0, row_start:keys_used, :]
        scores = jnp.dot(query, kt_ref[:, 0:keys_used], preferred_element_type=jnp.float32)
        query_index = row_start + lax.broadcasted_iota(jnp.int32, (block, 1), 0)
        limit = jnp.minimum(query_index, length - 1)
        key_index = row_start + lax.broadcasted_iota(jnp.int32, (1, block), 1)
        diag = jnp.where(key_index <= limit, scores[:, row_start:], jnp.float32(-1e30))
        scores = jnp.concatenate([scores[:, :row_start], diag], axis=1) if row_start else diag
        highest = jnp.max(scores, axis=-1, keepdims=True)
        weights = jnp.exp((scores - highest) * scale).astype(jnp.bfloat16)
        both = jnp.dot(weights, vx_ref[0:keys_used, :], preferred_element_type=jnp.float32)
        result = both[:, :head_dim] / both[:, head_dim : head_dim + 1]
        result = jnp.where(query_index < length, result, jnp.float32(0.0))
        o_ref[0, row_start:keys_used, :] = result.astype(o_ref.dtype)


def attend(heads_first, keys_t, values_ext, length, head_dim, block=256):
    heads, prompt, _ = heads_first.shape
    grid_spec = pltpu.PrefetchScalarGridSpec(
        num_scalar_prefetch=1,
        grid=(heads,),
        in_specs=[
            pl.BlockSpec((1, prompt, head_dim), lambda h, lens: (h, 0, 0)),
            pl.BlockSpec((head_dim, prompt), lambda h, lens: (0, 0)),
            pl.BlockSpec((prompt, 2 * head_dim), lambda h, lens: (0, 0)),
        ],
        out_specs=pl.BlockSpec((1, prompt, head_dim), lambda h, lens: (h, 0, 0)),
    )
    return pl.pallas_call(
        functools.partial(attention_kernel, block, head_dim),
        grid_spec=grid_spec,
        out_shape=jax.ShapeDtypeStruct((heads, prompt, head_dim), jnp.bfloat16),
        compiler_params=pltpu.CompilerParams(dimension_semantics=("arbitrary",)),
    )(length, heads_first, keys_t, values_ext)


def per_device(queries, text_kv, image_rows, row_request, row_position, prompt_lengths, kv_weight):
    groups = lax.axis_size("req")
    own_rows = image_rows.shape[0]
    capacity = 2 * own_rows // groups
    prompt = queries.shape[1]
    head_dim = queries.shape[3]
    width = 2 * head_dim
    me = lax.axis_index("tp")
    partial = jnp.einsum("rd,dhc->hrc", image_rows, kv_weight, preferred_element_type=jnp.bfloat16)
    heads = partial.shape[0]
    own_weight = lax.dynamic_index_in_dim(kv_weight, me, axis=1, keepdims=False)
    summed = jnp.dot(image_rows, own_weight, preferred_element_type=jnp.float32)
    for shift in range(1, heads):
        outgoing = lax.dynamic_index_in_dim(partial, (me + shift) % heads, axis=0, keepdims=False)
        incoming = lax.ppermute(
            outgoing, "tp", perm=[(i, (i + shift) % heads) for i in range(heads)]
        )
        summed = summed + incoming.astype(jnp.float32)
    image_kv = rotate_keys(summed, row_position, head_dim)
    one_hot = (row_request[:, None] == jnp.arange(groups, dtype=jnp.int32)[None, :]).astype(
        jnp.int32
    )
    before = jnp.cumsum(one_hot, axis=0) - one_hot
    slot_index = jnp.sum(before * one_hot, axis=1)
    target = row_request * capacity + slot_index
    slots = groups * capacity
    pick = (target[None, :] == jnp.arange(slots, dtype=jnp.int32)[:, None]).astype(jnp.bfloat16)
    send_kv = jnp.dot(pick, image_kv, preferred_element_type=jnp.float32).astype(jnp.bfloat16)
    pos_f = row_position.astype(jnp.float32) + 1.0
    digits = jnp.stack([jnp.floor(pos_f / 16.0), pos_f - 16.0 * jnp.floor(pos_f / 16.0)], axis=1)
    send_pos = jnp.dot(pick.astype(jnp.float32), digits, precision=lax.Precision.HIGHEST)
    tail = send_pos.reshape(groups, 2 * capacity).astype(jnp.bfloat16)
    tail = jnp.pad(tail, ((0, 0), (0, 128 - 2 * capacity)))
    packet = jnp.concatenate([send_kv.reshape(groups, capacity * width), tail], axis=1)
    text = text_kv[0, :, 0, :]
    text_keys_t = jnp.transpose(text[:, :head_dim])
    ones = jnp.ones((prompt, head_dim), text.dtype)
    text_values_ext = jnp.concatenate([text[:, head_dim:], ones], axis=1)
    got = lax.all_to_all(packet, "req", split_axis=0, concat_axis=0, tiled=True)
    got_kv = got[:, : capacity * width].reshape(slots, width)
    got_digits = got[:, capacity * width : capacity * width + 2 * capacity].astype(jnp.int32)
    got_digits = got_digits.reshape(slots, 2)
    places = got_digits[:, 0] * 16 + got_digits[:, 1] - 1
    match = places[None, :] == jnp.arange(prompt, dtype=jnp.int32)[:, None]
    place = match.astype(jnp.bfloat16)
    hit = jnp.any(match, axis=1)
    image_keys_t = jnp.einsum(
        "sd,ps->dp", got_kv[:, :head_dim], place, preferred_element_type=jnp.float32
    ).astype(jnp.bfloat16)
    image_values = jnp.dot(place, got_kv[:, head_dim:], preferred_element_type=jnp.float32)
    keys_t = jnp.where(hit[None, :], image_keys_t, text_keys_t)
    values_ext = jnp.where(
        hit[:, None], jnp.concatenate([image_values.astype(jnp.bfloat16), ones], axis=1),
        text_values_ext,
    )
    heads_first = jnp.transpose(queries[0], (1, 0, 2))
    out = attend(heads_first, keys_t, values_ext, prompt_lengths, head_dim)
    return jnp.transpose(out, (1, 0, 2))[None]


def solution(mesh):
    in_specs = (
        P("req", None, "tp", None),
        P("req", None, "tp", None),
        P("req", "tp"),
        P("req"),
        P("req"),
        P("req"),
        P("tp", None, None),
    )
    out_specs = P("req", None, "tp", None)
    return jax.shard_map(
        per_device, mesh=mesh, in_specs=in_specs, out_specs=out_specs, check_vma=False
    )
```

```python
import functools
import math

import jax
import jax.numpy as jnp
from jax import lax
from jax.experimental import pallas as pl
from jax.experimental.pallas import tpu as pltpu
from jax.sharding import PartitionSpec as P


def rotate_keys(summed, positions, head_dim):
    half = head_dim // 2
    freqs = jnp.exp(jnp.arange(half, dtype=jnp.float32) * (-2.0 * math.log(1000000.0) / head_dim))
    angles = positions.astype(jnp.float32)[:, None] * freqs[None, :]
    cosine = jnp.cos(angles)
    sine = jnp.sin(angles)
    first = summed[..., :half]
    second = summed[..., half:head_dim]
    rotated = jnp.concatenate(
        [first * cosine - second * sine, second * cosine + first * sine, summed[..., head_dim:]],
        axis=-1,
    )
    return rotated.astype(jnp.bfloat16)


def attention_kernel(block, head_dim, len_ref, q_ref, kt_ref, vx_ref, o_ref):
    prompt = q_ref.shape[1]
    length = len_ref[0]
    scale = head_dim ** (-0.5)
    for index in range(prompt // block):
        row_start = index * block
        keys_used = row_start + block
        query = q_ref[0, row_start:keys_used, :]
        scores = jnp.dot(query, kt_ref[:, 0:keys_used], preferred_element_type=jnp.float32)
        query_index = row_start + lax.broadcasted_iota(jnp.int32, (block, 1), 0)
        limit = jnp.minimum(query_index, length - 1)
        key_index = row_start + lax.broadcasted_iota(jnp.int32, (1, block), 1)
        diag = jnp.where(key_index <= limit, scores[:, row_start:], jnp.float32(-1e30))
        scores = jnp.concatenate([scores[:, :row_start], diag], axis=1) if row_start else diag
        highest = jnp.max(scores, axis=-1, keepdims=True)
        weights = jnp.exp((scores - highest) * scale).astype(jnp.bfloat16)
        both = jnp.dot(weights, vx_ref[0:keys_used, :], preferred_element_type=jnp.float32)
        result = both[:, :head_dim] / both[:, head_dim : head_dim + 1]
        result = jnp.where(query_index < length, result, jnp.float32(0.0))
        o_ref[0, row_start:keys_used, :] = result.astype(o_ref.dtype)


def attend(heads_first, keys_t, values_ext, length, head_dim, block=256):
    heads, prompt, _ = heads_first.shape
    grid_spec = pltpu.PrefetchScalarGridSpec(
        num_scalar_prefetch=1,
        grid=(heads,),
        in_specs=[
            pl.BlockSpec((1, prompt, head_dim), lambda h, lens: (h, 0, 0)),
            pl.BlockSpec((head_dim, prompt), lambda h, lens: (0, 0)),
            pl.BlockSpec((prompt, 2 * head_dim), lambda h, lens: (0, 0)),
        ],
        out_specs=pl.BlockSpec((1, prompt, head_dim), lambda h, lens: (h, 0, 0)),
    )
    return pl.pallas_call(
        functools.partial(attention_kernel, block, head_dim),
        grid_spec=grid_spec,
        out_shape=jax.ShapeDtypeStruct((heads, prompt, head_dim), jnp.bfloat16),
        compiler_params=pltpu.CompilerParams(dimension_semantics=("arbitrary",)),
    )(length, heads_first, keys_t, values_ext)


def torus_factors(groups):
    cores = 2 if groups % 2 == 0 else 1
    rows = 4 if (groups // cores) % 4 == 0 else 1
    return rows, groups // (rows * cores), cores


def staged_exchange(packet, factors):
    ny, nz, nc = factors
    groups = ny * nz * nc
    width = packet.shape[1]

    def shifted(axis, step):
        pairs = []
        for i in range(groups):
            coord = [i // (nz * nc), (i // nc) % nz, i % nc]
            coord[axis] = (coord[axis] + step) % factors[axis]
            pairs.append((i, (coord[0] * nz + coord[1]) * nc + coord[2]))
        return pairs

    buf = packet.reshape(ny, nz, nc, width)
    pieces = [buf[:, :, 0]]
    for step in range(1, nc):
        pieces.append(lax.ppermute(buf[:, :, step], "req", perm=shifted(2, step)))
    buf = jnp.stack(pieces, axis=2)
    pieces = [buf[:, 0]]
    for step in range(1, nz):
        pieces.append(lax.ppermute(buf[:, step], "req", perm=shifted(1, step)))
    buf = jnp.stack(pieces, axis=1)
    pieces = [buf[0]]
    for step in range(1, ny):
        pieces.append(lax.ppermute(buf[step], "req", perm=shifted(0, step)))
    return jnp.stack(pieces, axis=0).reshape(groups, width)


def per_device(queries, text_kv, image_rows, row_request, row_position, prompt_lengths, kv_weight):
    groups = lax.axis_size("req")
    own_rows = image_rows.shape[0]
    capacity = 2 * own_rows // groups
    prompt = queries.shape[1]
    head_dim = queries.shape[3]
    width = 2 * head_dim
    me = lax.axis_index("tp")
    partial = jnp.einsum("rd,dhc->hrc", image_rows, kv_weight, preferred_element_type=jnp.bfloat16)
    heads = partial.shape[0]
    own_weight = lax.dynamic_index_in_dim(kv_weight, me, axis=1, keepdims=False)
    summed = jnp.dot(image_rows, own_weight, preferred_element_type=jnp.float32)
    for shift in range(1, heads):
        outgoing = lax.dynamic_index_in_dim(partial, (me + shift) % heads, axis=0, keepdims=False)
        incoming = lax.ppermute(
            outgoing, "tp", perm=[(i, (i + shift) % heads) for i in range(heads)]
        )
        summed = summed + incoming.astype(jnp.float32)
    image_kv = rotate_keys(summed, row_position, head_dim)
    one_hot = (row_request[:, None] == jnp.arange(groups, dtype=jnp.int32)[None, :]).astype(
        jnp.int32
    )
    before = jnp.cumsum(one_hot, axis=0) - one_hot
    slot_index = jnp.sum(before * one_hot, axis=1)
    ny, nz, nc = factors = torus_factors(groups)
    here = lax.axis_index("req")
    relative = (
        ((row_request // (nz * nc) - here // (nz * nc)) % ny * nz
         + (row_request // nc - here // nc) % nz) * nc
        + (row_request - here) % nc
    )
    target = relative * capacity + slot_index
    slots = groups * capacity
    pick = (target[None, :] == jnp.arange(slots, dtype=jnp.int32)[:, None]).astype(jnp.bfloat16)
    send_kv = jnp.dot(pick, image_kv, preferred_element_type=jnp.float32).astype(jnp.bfloat16)
    pos_f = row_position.astype(jnp.float32) + 1.0
    digits = jnp.stack([jnp.floor(pos_f / 16.0), pos_f - 16.0 * jnp.floor(pos_f / 16.0)], axis=1)
    send_pos = jnp.dot(pick.astype(jnp.float32), digits, precision=lax.Precision.HIGHEST)
    tail = send_pos.reshape(groups, 2 * capacity).astype(jnp.bfloat16)
    tail = jnp.pad(tail, ((0, 0), (0, 128 - 2 * capacity)))
    packet = jnp.concatenate([send_kv.reshape(groups, capacity * width), tail], axis=1)
    text = text_kv[0, :, 0, :]
    text_keys_t = jnp.transpose(text[:, :head_dim])
    ones = jnp.ones((prompt, head_dim), text.dtype)
    text_values_ext = jnp.concatenate([text[:, head_dim:], ones], axis=1)
    got = staged_exchange(packet, factors)
    got_kv = got[:, : capacity * width].reshape(slots, width)
    got_digits = got[:, capacity * width : capacity * width + 2 * capacity].astype(jnp.int32)
    got_digits = got_digits.reshape(slots, 2)
    places = got_digits[:, 0] * 16 + got_digits[:, 1] - 1
    match = places[None, :] == jnp.arange(prompt, dtype=jnp.int32)[:, None]
    place = match.astype(jnp.bfloat16)
    hit = jnp.any(match, axis=1)
    image_keys_t = jnp.einsum(
        "sd,ps->dp", got_kv[:, :head_dim], place, preferred_element_type=jnp.float32
    ).astype(jnp.bfloat16)
    image_values = jnp.dot(place, got_kv[:, head_dim:], preferred_element_type=jnp.float32)
    keys_t = jnp.where(hit[None, :], image_keys_t, text_keys_t)
    values_ext = jnp.where(
        hit[:, None], jnp.concatenate([image_values.astype(jnp.bfloat16), ones], axis=1),
        text_values_ext,
    )
    heads_first = jnp.transpose(queries[0], (1, 0, 2))
    out = attend(heads_first, keys_t, values_ext, prompt_lengths, head_dim)
    return jnp.transpose(out, (1, 0, 2))[None]


def solution(mesh):
    in_specs = (
        P("req", None, "tp", None),
        P("req", None, "tp", None),
        P("req", "tp"),
        P("req"),
        P("req"),
        P("req"),
        P("tp", None, None),
    )
    out_specs = P("req", None, "tp", None)
    return jax.shard_map(
        per_device, mesh=mesh, in_specs=in_specs, out_specs=out_specs, check_vma=False
    )
```

```python
import functools
import math

import jax
import jax.numpy as jnp
from jax import lax
from jax.experimental import pallas as pl
from jax.experimental.pallas import tpu as pltpu
from jax.sharding import PartitionSpec as P


def rotate_keys(summed, positions, head_dim):
    half = head_dim // 2
    freqs = jnp.exp(jnp.arange(half, dtype=jnp.float32) * (-2.0 * math.log(1000000.0) / head_dim))
    angles = positions.astype(jnp.float32)[:, None] * freqs[None, :]
    cosine = jnp.cos(angles)
    sine = jnp.sin(angles)
    first = summed[..., :half]
    second = summed[..., half:head_dim]
    rotated = jnp.concatenate(
        [first * cosine - second * sine, second * cosine + first * sine, summed[..., head_dim:]],
        axis=-1,
    )
    return rotated.astype(jnp.bfloat16)


def attention_kernel(block, head_dim, len_ref, q_ref, kv_ref, o_ref, vx_ref):
    prompt = q_ref.shape[1]
    length = len_ref[0]
    scale = head_dim ** (-0.5)

    @pl.when(pl.program_id(0) == 0)
    def _():
        vx_ref[:, :head_dim] = kv_ref[:, head_dim:]
        vx_ref[:, head_dim:] = jnp.ones((prompt, head_dim), vx_ref.dtype)

    for index in range(prompt // block):
        row_start = index * block
        keys_used = row_start + block
        query = q_ref[0, row_start:keys_used, :]
        scores = lax.dot_general(
            query, kv_ref[0:keys_used, 0:head_dim], (((1,), (1,)), ((), ())),
            preferred_element_type=jnp.float32,
        )
        query_index = row_start + lax.broadcasted_iota(jnp.int32, (block, 1), 0)
        limit = jnp.minimum(query_index, length - 1)
        key_index = row_start + lax.broadcasted_iota(jnp.int32, (1, block), 1)
        diag = jnp.where(key_index <= limit, scores[:, row_start:], jnp.float32(-1e30))
        scores = jnp.concatenate([scores[:, :row_start], diag], axis=1) if row_start else diag
        highest = jnp.max(scores, axis=-1, keepdims=True)
        weights = jnp.exp((scores - highest) * scale).astype(jnp.bfloat16)
        both = jnp.dot(weights, vx_ref[0:keys_used, :], preferred_element_type=jnp.float32)
        result = both[:, :head_dim] / both[:, head_dim : head_dim + 1]
        result = jnp.where(query_index < length, result, jnp.float32(0.0))
        o_ref[0, row_start:keys_used, :] = result.astype(o_ref.dtype)


def attend(heads_first, prompt_kv, length, head_dim, block=256):
    heads, prompt, _ = heads_first.shape
    grid_spec = pltpu.PrefetchScalarGridSpec(
        num_scalar_prefetch=1,
        grid=(heads,),
        in_specs=[
            pl.BlockSpec((1, prompt, head_dim), lambda h, lens: (h, 0, 0)),
            pl.BlockSpec((prompt, 2 * head_dim), lambda h, lens: (0, 0)),
        ],
        out_specs=pl.BlockSpec((1, prompt, head_dim), lambda h, lens: (h, 0, 0)),
        scratch_shapes=[pltpu.VMEM((prompt, 2 * head_dim), jnp.bfloat16)],
    )
    return pl.pallas_call(
        functools.partial(attention_kernel, block, head_dim),
        grid_spec=grid_spec,
        out_shape=jax.ShapeDtypeStruct((heads, prompt, head_dim), jnp.bfloat16),
        compiler_params=pltpu.CompilerParams(dimension_semantics=("arbitrary",)),
    )(length, heads_first, prompt_kv)


def per_device(queries, text_kv, image_rows, row_request, row_position, prompt_lengths, kv_weight):
    groups = lax.axis_size("req")
    own_rows = image_rows.shape[0]
    capacity = 2 * own_rows // groups
    prompt = queries.shape[1]
    head_dim = queries.shape[3]
    width = 2 * head_dim
    me = lax.axis_index("tp")
    partial = jnp.einsum("rd,dhc->hrc", image_rows, kv_weight, preferred_element_type=jnp.bfloat16)
    heads = partial.shape[0]
    own_weight = lax.dynamic_index_in_dim(kv_weight, me, axis=1, keepdims=False)
    summed = jnp.dot(image_rows, own_weight, preferred_element_type=jnp.float32)
    for shift in range(1, heads):
        outgoing = lax.dynamic_index_in_dim(partial, (me + shift) % heads, axis=0, keepdims=False)
        incoming = lax.ppermute(
            outgoing, "tp", perm=[(i, (i + shift) % heads) for i in range(heads)]
        )
        summed = summed + incoming.astype(jnp.float32)
    image_kv = rotate_keys(summed, row_position, head_dim)
    one_hot = (row_request[:, None] == jnp.arange(groups, dtype=jnp.int32)[None, :]).astype(
        jnp.int32
    )
    before = jnp.cumsum(one_hot, axis=0) - one_hot
    slot_index = jnp.sum(before * one_hot, axis=1)
    target = row_request * capacity + slot_index
    slots = groups * capacity
    pick = (target[None, :] == jnp.arange(slots, dtype=jnp.int32)[:, None]).astype(jnp.bfloat16)
    send_kv = jnp.dot(pick, image_kv, preferred_element_type=jnp.float32).astype(jnp.bfloat16)
    pos_f = row_position.astype(jnp.float32) + 1.0
    digits = jnp.stack([jnp.floor(pos_f / 16.0), pos_f - 16.0 * jnp.floor(pos_f / 16.0)], axis=1)
    send_pos = jnp.dot(pick.astype(jnp.float32), digits, precision=lax.Precision.HIGHEST)
    tail = send_pos.reshape(groups, 2 * capacity).astype(jnp.bfloat16)
    tail = jnp.pad(tail, ((0, 0), (0, 128 - 2 * capacity)))
    packet = jnp.concatenate([send_kv.reshape(groups, capacity * width), tail], axis=1)
    got = lax.all_to_all(packet, "req", split_axis=0, concat_axis=0, tiled=True)
    got_kv = got[:, : capacity * width].reshape(slots, width)
    got_digits = got[:, capacity * width : capacity * width + 2 * capacity].astype(jnp.int32)
    got_digits = got_digits.reshape(slots, 2)
    places = got_digits[:, 0] * 16 + got_digits[:, 1] - 1
    match = places[None, :] == jnp.arange(prompt, dtype=jnp.int32)[:, None]
    placed = jnp.dot(match.astype(jnp.bfloat16), got_kv, preferred_element_type=jnp.float32)
    hit = jnp.any(match, axis=1)
    prompt_kv = jnp.where(hit[:, None], placed.astype(jnp.bfloat16), text_kv[0, :, 0, :])
    heads_first = jnp.transpose(queries[0], (1, 0, 2))
    out = attend(heads_first, prompt_kv, prompt_lengths, head_dim)
    return jnp.transpose(out, (1, 0, 2))[None]


def solution(mesh):
    in_specs = (
        P("req", None, "tp", None),
        P("req", None, "tp", None),
        P("req", "tp"),
        P("req"),
        P("req"),
        P("req"),
        P("tp", None, None),
    )
    out_specs = P("req", None, "tp", None)
    return jax.shard_map(
        per_device, mesh=mesh, in_specs=in_specs, out_specs=out_specs, check_vma=False
    )
```

```python
import functools
import math

import jax
import jax.numpy as jnp
from jax import lax
from jax.experimental import pallas as pl
from jax.experimental.pallas import tpu as pltpu
from jax.sharding import PartitionSpec as P


def rotate_keys(summed, positions, head_dim):
    half = head_dim // 2
    freqs = jnp.exp(jnp.arange(half, dtype=jnp.float32) * (-2.0 * math.log(1000000.0) / head_dim))
    angles = positions.astype(jnp.float32)[:, None] * freqs[None, :]
    cosine = jnp.cos(angles)
    sine = jnp.sin(angles)
    first = summed[..., :half]
    second = summed[..., half:head_dim]
    rotated = jnp.concatenate(
        [first * cosine - second * sine, second * cosine + first * sine, summed[..., head_dim:]],
        axis=-1,
    )
    return rotated.astype(jnp.bfloat16)


def attention_kernel(block, head_dim, group, len_ref, q_ref, kv_ref, o_ref, vx_ref):
    prompt = q_ref.shape[1]
    length = len_ref[0]
    scale = head_dim ** (-0.5)

    @pl.when(pl.program_id(0) == 0)
    def _():
        vx_ref[:, :head_dim] = kv_ref[:, head_dim:]
        vx_ref[:, head_dim:] = jnp.ones((prompt, head_dim), vx_ref.dtype)

    for index in range(prompt // block):
        row_start = index * block
        keys_used = row_start + block
        query = jnp.concatenate([q_ref[g, row_start:keys_used, :] for g in range(group)], axis=0)
        scores = lax.dot_general(
            query, kv_ref[0:keys_used, 0:head_dim], (((1,), (1,)), ((), ())),
            preferred_element_type=jnp.float32,
        )
        query_index = row_start + lax.broadcasted_iota(jnp.int32, (group * block, 1), 0) % block
        limit = jnp.minimum(query_index, length - 1)
        key_index = row_start + lax.broadcasted_iota(jnp.int32, (1, block), 1)
        diag = jnp.where(key_index <= limit, scores[:, row_start:], jnp.float32(-1e30))
        scores = jnp.concatenate([scores[:, :row_start], diag], axis=1) if row_start else diag
        highest = jnp.max(scores, axis=-1, keepdims=True)
        weights = jnp.exp((scores - highest) * scale).astype(jnp.bfloat16)
        both = jnp.dot(weights, vx_ref[0:keys_used, :], preferred_element_type=jnp.float32)
        result = both[:, :head_dim] / both[:, head_dim : head_dim + 1]
        result = jnp.where(query_index < length, result, jnp.float32(0.0)).astype(o_ref.dtype)
        for g in range(group):
            o_ref[g, row_start:keys_used, :] = result[g * block : (g + 1) * block]


def attend(heads_first, prompt_kv, length, head_dim, block=256):
    heads, prompt, _ = heads_first.shape
    group = math.gcd(heads, 3)
    grid_spec = pltpu.PrefetchScalarGridSpec(
        num_scalar_prefetch=1,
        grid=(heads // group,),
        in_specs=[
            pl.BlockSpec((group, prompt, head_dim), lambda h, lens: (h, 0, 0)),
            pl.BlockSpec((prompt, 2 * head_dim), lambda h, lens: (0, 0)),
        ],
        out_specs=pl.BlockSpec((group, prompt, head_dim), lambda h, lens: (h, 0, 0)),
        scratch_shapes=[pltpu.VMEM((prompt, 2 * head_dim), jnp.bfloat16)],
    )
    return pl.pallas_call(
        functools.partial(attention_kernel, block, head_dim, group),
        grid_spec=grid_spec,
        out_shape=jax.ShapeDtypeStruct((heads, prompt, head_dim), jnp.bfloat16),
        compiler_params=pltpu.CompilerParams(dimension_semantics=("arbitrary",)),
    )(length, heads_first, prompt_kv)


def per_device(queries, text_kv, image_rows, row_request, row_position, prompt_lengths, kv_weight):
    groups = lax.axis_size("req")
    own_rows = image_rows.shape[0]
    capacity = 2 * own_rows // groups
    prompt = queries.shape[1]
    head_dim = queries.shape[3]
    width = 2 * head_dim
    me = lax.axis_index("tp")
    partial = jnp.einsum("rd,dhc->hrc", image_rows, kv_weight, preferred_element_type=jnp.bfloat16)
    heads = partial.shape[0]
    own_weight = lax.dynamic_index_in_dim(kv_weight, me, axis=1, keepdims=False)
    summed = jnp.dot(image_rows, own_weight, preferred_element_type=jnp.float32)
    for shift in range(1, heads):
        outgoing = lax.dynamic_index_in_dim(partial, (me + shift) % heads, axis=0, keepdims=False)
        incoming = lax.ppermute(
            outgoing, "tp", perm=[(i, (i + shift) % heads) for i in range(heads)]
        )
        summed = summed + incoming.astype(jnp.float32)
    image_kv = rotate_keys(summed, row_position, head_dim)
    one_hot = (row_request[:, None] == jnp.arange(groups, dtype=jnp.int32)[None, :]).astype(
        jnp.int32
    )
    before = jnp.cumsum(one_hot, axis=0) - one_hot
    slot_index = jnp.sum(before * one_hot, axis=1)
    target = row_request * capacity + slot_index
    slots = groups * capacity
    pick = (target[None, :] == jnp.arange(slots, dtype=jnp.int32)[:, None]).astype(jnp.bfloat16)
    send_kv = jnp.dot(pick, image_kv, preferred_element_type=jnp.float32).astype(jnp.bfloat16)
    pos_f = row_position.astype(jnp.float32) + 1.0
    digits = jnp.stack([jnp.floor(pos_f / 16.0), pos_f - 16.0 * jnp.floor(pos_f / 16.0)], axis=1)
    send_pos = jnp.dot(pick.astype(jnp.float32), digits, precision=lax.Precision.HIGHEST)
    tail = send_pos.reshape(groups, 2 * capacity).astype(jnp.bfloat16)
    tail = jnp.pad(tail, ((0, 0), (0, 128 - 2 * capacity)))
    packet = jnp.concatenate([send_kv.reshape(groups, capacity * width), tail], axis=1)
    got = lax.all_to_all(packet, "req", split_axis=0, concat_axis=0, tiled=True)
    got_kv = got[:, : capacity * width].reshape(slots, width)
    got_digits = got[:, capacity * width : capacity * width + 2 * capacity].astype(jnp.int32)
    got_digits = got_digits.reshape(slots, 2)
    places = got_digits[:, 0] * 16 + got_digits[:, 1] - 1
    match = places[None, :] == jnp.arange(prompt, dtype=jnp.int32)[:, None]
    placed = jnp.dot(match.astype(jnp.bfloat16), got_kv, preferred_element_type=jnp.float32)
    hit = jnp.any(match, axis=1)
    prompt_kv = jnp.where(hit[:, None], placed.astype(jnp.bfloat16), text_kv[0, :, 0, :])
    heads_first = jnp.transpose(queries[0], (1, 0, 2))
    out = attend(heads_first, prompt_kv, prompt_lengths, head_dim)
    return jnp.transpose(out, (1, 0, 2))[None]


def solution(mesh):
    in_specs = (
        P("req", None, "tp", None),
        P("req", None, "tp", None),
        P("req", "tp"),
        P("req"),
        P("req"),
        P("req"),
        P("tp", None, None),
    )
    out_specs = P("req", None, "tp", None)
    return jax.shard_map(
        per_device, mesh=mesh, in_specs=in_specs, out_specs=out_specs, check_vma=False
    )
```

```python
import functools
import math

import jax
import jax.numpy as jnp
from jax import lax
from jax.experimental import pallas as pl
from jax.experimental.pallas import tpu as pltpu
from jax.sharding import PartitionSpec as P


def rotate_keys(summed, positions, head_dim):
    half = head_dim // 2
    freqs = jnp.exp(jnp.arange(half, dtype=jnp.float32) * (-2.0 * math.log(1000000.0) / head_dim))
    angles = positions.astype(jnp.float32)[:, None] * freqs[None, :]
    cosine = jnp.cos(angles)
    sine = jnp.sin(angles)
    first = summed[..., :half]
    second = summed[..., half:head_dim]
    rotated = jnp.concatenate(
        [first * cosine - second * sine, second * cosine + first * sine, summed[..., head_dim:]],
        axis=-1,
    )
    return rotated.astype(jnp.bfloat16)


def attention_kernel(block, head_dim, group, len_ref, q_ref, kv_ref, o_ref, vx_ref):
    prompt = q_ref.shape[1]
    length = len_ref[0]
    scale = head_dim ** (-0.5)

    @pl.when(pl.program_id(0) == 0)
    def _():
        vx_ref[:, :head_dim] = kv_ref[:, head_dim:]
        vx_ref[:, head_dim:] = jnp.ones((prompt, head_dim), vx_ref.dtype)

    for index in range(prompt // block):
        row_start = index * block
        keys_used = row_start + block
        query = jnp.concatenate([q_ref[g, row_start:keys_used, :] for g in range(group)], axis=0)
        scores = lax.dot_general(
            query, kv_ref[0:keys_used, 0:head_dim], (((1,), (1,)), ((), ())),
            preferred_element_type=jnp.float32,
        )
        query_index = row_start + lax.broadcasted_iota(jnp.int32, (group * block, 1), 0) % block
        limit = jnp.minimum(query_index, length - 1)
        key_index = row_start + lax.broadcasted_iota(jnp.int32, (1, block), 1)
        diag = jnp.where(key_index <= limit, scores[:, row_start:], jnp.float32(-1e30))
        scores = jnp.concatenate([scores[:, :row_start], diag], axis=1) if row_start else diag
        highest = jnp.max(scores, axis=-1, keepdims=True)
        weights = jnp.exp((scores - highest) * scale).astype(jnp.bfloat16)
        both = jnp.dot(weights, vx_ref[0:keys_used, :], preferred_element_type=jnp.float32)
        result = both[:, :head_dim] / both[:, head_dim : head_dim + 1]
        result = jnp.where(query_index < length, result, jnp.float32(0.0)).astype(o_ref.dtype)
        for g in range(group):
            o_ref[g, row_start:keys_used, :] = result[g * block : (g + 1) * block]


def attend(heads_first, prompt_kv, length, head_dim, block=256):
    heads, prompt, _ = heads_first.shape
    group = math.gcd(heads, 3)
    grid_spec = pltpu.PrefetchScalarGridSpec(
        num_scalar_prefetch=1,
        grid=(heads // group,),
        in_specs=[
            pl.BlockSpec((group, prompt, head_dim), lambda h, lens: (h, 0, 0)),
            pl.BlockSpec((prompt, 2 * head_dim), lambda h, lens: (0, 0)),
        ],
        out_specs=pl.BlockSpec((group, prompt, head_dim), lambda h, lens: (h, 0, 0)),
        scratch_shapes=[pltpu.VMEM((prompt, 2 * head_dim), jnp.bfloat16)],
    )
    return pl.pallas_call(
        functools.partial(attention_kernel, block, head_dim, group),
        grid_spec=grid_spec,
        out_shape=jax.ShapeDtypeStruct((heads, prompt, head_dim), jnp.bfloat16),
        compiler_params=pltpu.CompilerParams(dimension_semantics=("arbitrary",)),
    )(length, heads_first, prompt_kv)


def per_device(queries, text_kv, image_rows, row_request, row_position, prompt_lengths, kv_weight):
    groups = lax.axis_size("req")
    own_rows = image_rows.shape[0]
    capacity = 2 * own_rows // groups
    prompt = queries.shape[1]
    head_dim = queries.shape[3]
    width = 2 * head_dim
    me = lax.axis_index("tp")
    partial = jnp.einsum("rd,dhc->hrc", image_rows, kv_weight, preferred_element_type=jnp.bfloat16)
    heads = partial.shape[0]
    own_weight = lax.dynamic_index_in_dim(kv_weight, me, axis=1, keepdims=False)
    summed = jnp.dot(image_rows, own_weight, preferred_element_type=jnp.float32)
    for shift in range(1, heads):
        outgoing = lax.dynamic_index_in_dim(partial, (me + shift) % heads, axis=0, keepdims=False)
        incoming = lax.ppermute(
            outgoing, "tp", perm=[(i, (i + shift) % heads) for i in range(heads)]
        )
        summed = summed + incoming.astype(jnp.float32)
    image_kv = rotate_keys(summed, row_position, head_dim)
    one_hot = (row_request[:, None] == jnp.arange(groups, dtype=jnp.int32)[None, :]).astype(
        jnp.int32
    )
    before = jnp.cumsum(one_hot, axis=0) - one_hot
    slot_index = jnp.sum(before * one_hot, axis=1)
    target = row_request * capacity + slot_index
    slots = groups * capacity
    pick = (target[None, :] == jnp.arange(slots, dtype=jnp.int32)[:, None]).astype(jnp.bfloat16)
    send_kv = jnp.dot(pick, image_kv, preferred_element_type=jnp.float32).astype(jnp.bfloat16)
    pos_f = row_position.astype(jnp.float32) + 1.0
    digits = jnp.stack([jnp.floor(pos_f / 16.0), pos_f - 16.0 * jnp.floor(pos_f / 16.0)], axis=1)
    send_pos = jnp.dot(pick.astype(jnp.float32), digits, precision=lax.Precision.HIGHEST)
    tail = send_pos.reshape(groups, 2, capacity).astype(jnp.bfloat16)
    tail = jnp.pad(tail, ((0, 0), (0, 0), (0, 64 - capacity)))
    packet = jnp.concatenate([send_kv.reshape(groups, 2, capacity * width // 2), tail], axis=2)
    got = lax.all_to_all(packet, "req", split_axis=0, concat_axis=0, tiled=True)
    got_kv = got[:, :, : capacity * width // 2].reshape(slots, width)
    got_digits = got[:, :, capacity * width // 2 : capacity * width // 2 + capacity]
    got_digits = got_digits.astype(jnp.int32).reshape(slots, 2)
    places = got_digits[:, 0] * 16 + got_digits[:, 1] - 1
    match = places[None, :] == jnp.arange(prompt, dtype=jnp.int32)[:, None]
    placed = jnp.dot(match.astype(jnp.bfloat16), got_kv, preferred_element_type=jnp.float32)
    hit = jnp.any(match, axis=1)
    prompt_kv = jnp.where(hit[:, None], placed.astype(jnp.bfloat16), text_kv[0, :, 0, :])
    heads_first = jnp.transpose(queries[0], (1, 0, 2))
    out = attend(heads_first, prompt_kv, prompt_lengths, head_dim)
    return jnp.transpose(out, (1, 0, 2))[None]


def solution(mesh):
    in_specs = (
        P("req", None, "tp", None),
        P("req", None, "tp", None),
        P("req", "tp"),
        P("req"),
        P("req"),
        P("req"),
        P("tp", None, None),
    )
    out_specs = P("req", None, "tp", None)
    return jax.shard_map(
        per_device, mesh=mesh, in_specs=in_specs, out_specs=out_specs, check_vma=False
    )
```

```python
import functools
import math

import jax
import jax.numpy as jnp
from jax import lax
from jax.experimental import pallas as pl
from jax.experimental.pallas import tpu as pltpu
from jax.sharding import PartitionSpec as P


def rotate_keys(summed, positions, head_dim):
    half = head_dim // 2
    freqs = jnp.exp(jnp.arange(half, dtype=jnp.float32) * (-2.0 * math.log(1000000.0) / head_dim))
    angles = positions.astype(jnp.float32)[:, None] * freqs[None, :]
    cosine = jnp.cos(angles)
    sine = jnp.sin(angles)
    first = summed[..., :half]
    second = summed[..., half:head_dim]
    rotated = jnp.concatenate(
        [first * cosine - second * sine, second * cosine + first * sine, summed[..., head_dim:]],
        axis=-1,
    )
    return rotated.astype(jnp.bfloat16)


def attention_kernel(block, head_dim, group, len_ref, q_ref, kv_ref, o_ref, vx_ref):
    prompt = kv_ref.shape[0]
    length = len_ref[0]
    scale = head_dim ** (-0.5)
    step = pl.program_id(1)

    @pl.when((pl.program_id(0) == 0) & (step == 0))
    def _():
        vx_ref[:, :head_dim] = kv_ref[:, head_dim:]
        vx_ref[:, head_dim:] = jnp.ones((prompt, head_dim), vx_ref.dtype)

    for index in range(prompt // block):
        row_start = index * block
        keys_used = row_start + block

        @pl.when(step == index)
        def _():
            query = jnp.concatenate([q_ref[g] for g in range(group)], axis=0)
            scores = lax.dot_general(
                query, kv_ref[0:keys_used, 0:head_dim], (((1,), (1,)), ((), ())),
                preferred_element_type=jnp.float32,
            )
            query_index = row_start + lax.broadcasted_iota(jnp.int32, (group * block, 1), 0) % block
            limit = jnp.minimum(query_index, length - 1)
            key_index = row_start + lax.broadcasted_iota(jnp.int32, (1, block), 1)
            diag = jnp.where(key_index <= limit, scores[:, row_start:], jnp.float32(-1e30))
            scores = jnp.concatenate([scores[:, :row_start], diag], axis=1) if row_start else diag
            highest = jnp.max(scores, axis=-1, keepdims=True)
            weights = jnp.exp((scores - highest) * scale).astype(jnp.bfloat16)
            both = jnp.dot(weights, vx_ref[0:keys_used, :], preferred_element_type=jnp.float32)
            result = both[:, :head_dim] / both[:, head_dim : head_dim + 1]
            result = jnp.where(query_index < length, result, jnp.float32(0.0)).astype(o_ref.dtype)
            for g in range(group):
                o_ref[g] = result[g * block : (g + 1) * block]


def attend(heads_first, prompt_kv, length, head_dim, block=256):
    heads, prompt, _ = heads_first.shape
    group = math.gcd(heads, 3)
    grid_spec = pltpu.PrefetchScalarGridSpec(
        num_scalar_prefetch=1,
        grid=(heads // group, prompt // block),
        in_specs=[
            pl.BlockSpec((group, block, head_dim), lambda h, i, lens: (h, i, 0)),
            pl.BlockSpec((prompt, 2 * head_dim), lambda h, i, lens: (0, 0)),
        ],
        out_specs=pl.BlockSpec((group, block, head_dim), lambda h, i, lens: (h, i, 0)),
        scratch_shapes=[pltpu.VMEM((prompt, 2 * head_dim), jnp.bfloat16)],
    )
    return pl.pallas_call(
        functools.partial(attention_kernel, block, head_dim, group),
        grid_spec=grid_spec,
        out_shape=jax.ShapeDtypeStruct((heads, prompt, head_dim), jnp.bfloat16),
        compiler_params=pltpu.CompilerParams(dimension_semantics=("arbitrary", "arbitrary")),
    )(length, heads_first, prompt_kv)


def per_device(queries, text_kv, image_rows, row_request, row_position, prompt_lengths, kv_weight):
    groups = lax.axis_size("req")
    own_rows = image_rows.shape[0]
    capacity = 2 * own_rows // groups
    prompt = queries.shape[1]
    head_dim = queries.shape[3]
    width = 2 * head_dim
    me = lax.axis_index("tp")
    partial = jnp.einsum("rd,dhc->hrc", image_rows, kv_weight, preferred_element_type=jnp.bfloat16)
    heads = partial.shape[0]
    own_weight = lax.dynamic_index_in_dim(kv_weight, me, axis=1, keepdims=False)
    summed = jnp.dot(image_rows, own_weight, preferred_element_type=jnp.float32)
    for shift in range(1, heads):
        outgoing = lax.dynamic_index_in_dim(partial, (me + shift) % heads, axis=0, keepdims=False)
        incoming = lax.ppermute(
            outgoing, "tp", perm=[(i, (i + shift) % heads) for i in range(heads)]
        )
        summed = summed + incoming.astype(jnp.float32)
    image_kv = rotate_keys(summed, row_position, head_dim)
    one_hot = (row_request[:, None] == jnp.arange(groups, dtype=jnp.int32)[None, :]).astype(
        jnp.int32
    )
    before = jnp.cumsum(one_hot, axis=0) - one_hot
    slot_index = jnp.sum(before * one_hot, axis=1)
    target = row_request * capacity + slot_index
    slots = groups * capacity
    pick = (target[None, :] == jnp.arange(slots, dtype=jnp.int32)[:, None]).astype(jnp.bfloat16)
    send_kv = jnp.dot(pick, image_kv, preferred_element_type=jnp.float32).astype(jnp.bfloat16)
    pos_f = row_position.astype(jnp.float32) + 1.0
    digits = jnp.stack([jnp.floor(pos_f / 16.0), pos_f - 16.0 * jnp.floor(pos_f / 16.0)], axis=1)
    send_pos = jnp.dot(pick.astype(jnp.float32), digits, precision=lax.Precision.HIGHEST)
    tail = send_pos.reshape(groups, 2, capacity).astype(jnp.bfloat16)
    tail = jnp.pad(tail, ((0, 0), (0, 0), (0, 64 - capacity)))
    packet = jnp.concatenate([send_kv.reshape(groups, 2, capacity * width // 2), tail], axis=2)
    got = lax.all_to_all(packet, "req", split_axis=0, concat_axis=0, tiled=True)
    got_kv = got[:, :, : capacity * width // 2].reshape(slots, width)
    got_digits = got[:, :, capacity * width // 2 : capacity * width // 2 + capacity]
    got_digits = got_digits.astype(jnp.int32).reshape(slots, 2)
    places = got_digits[:, 0] * 16 + got_digits[:, 1] - 1
    match = places[None, :] == jnp.arange(prompt, dtype=jnp.int32)[:, None]
    placed = jnp.dot(match.astype(jnp.bfloat16), got_kv, preferred_element_type=jnp.float32)
    hit = jnp.any(match, axis=1)
    prompt_kv = jnp.where(hit[:, None], placed.astype(jnp.bfloat16), text_kv[0, :, 0, :])
    heads_first = jnp.transpose(queries[0], (1, 0, 2))
    out = attend(heads_first, prompt_kv, prompt_lengths, head_dim)
    return jnp.transpose(out, (1, 0, 2))[None]


def solution(mesh):
    in_specs = (
        P("req", None, "tp", None),
        P("req", None, "tp", None),
        P("req", "tp"),
        P("req"),
        P("req"),
        P("req"),
        P("tp", None, None),
    )
    out_specs = P("req", None, "tp", None)
    return jax.shard_map(
        per_device, mesh=mesh, in_specs=in_specs, out_specs=out_specs, check_vma=False
    )
```

```python
import functools
import math

import jax
import jax.numpy as jnp
from jax import lax
from jax.experimental import pallas as pl
from jax.experimental.pallas import tpu as pltpu
from jax.sharding import PartitionSpec as P


def rotate_keys(summed, positions, head_dim):
    half = head_dim // 2
    freqs = jnp.exp(jnp.arange(half, dtype=jnp.float32) * (-2.0 * math.log(1000000.0) / head_dim))
    angles = positions.astype(jnp.float32)[:, None] * freqs[None, :]
    cosine = jnp.cos(angles)
    sine = jnp.sin(angles)
    first = summed[..., :half]
    second = summed[..., half:head_dim]
    rotated = jnp.concatenate(
        [first * cosine - second * sine, second * cosine + first * sine, summed[..., head_dim:]],
        axis=-1,
    )
    return rotated.astype(jnp.bfloat16)


def attention_kernel(block, head_dim, group, len_ref, q_ref, kv_ref, o_ref, vx_ref):
    prompt = q_ref.shape[1]
    length = len_ref[0]
    scale = head_dim ** (-0.5)

    @pl.when(pl.program_id(0) == 0)
    def _():
        vx_ref[:, :head_dim] = kv_ref[:, head_dim:]
        vx_ref[:, head_dim:] = jnp.ones((prompt, head_dim), vx_ref.dtype)

    for index in range(prompt // block):
        row_start = index * block
        keys_used = row_start + block
        query = jnp.concatenate([q_ref[g, row_start:keys_used, :] for g in range(group)], axis=0)
        scores = lax.dot_general(
            query, kv_ref[0:keys_used, 0:head_dim], (((1,), (1,)), ((), ())),
            preferred_element_type=jnp.float32,
        )
        query_index = row_start + lax.broadcasted_iota(jnp.int32, (group * block, 1), 0) % block
        limit = jnp.minimum(query_index, length - 1)
        key_index = row_start + lax.broadcasted_iota(jnp.int32, (1, block), 1)
        diag = jnp.where(key_index <= limit, scores[:, row_start:], jnp.float32(-1e30))
        scores = jnp.concatenate([scores[:, :row_start], diag], axis=1) if row_start else diag
        highest = jnp.max(scores, axis=-1, keepdims=True)
        weights = jnp.exp((scores - highest) * scale).astype(jnp.bfloat16)
        both = jnp.dot(weights, vx_ref[0:keys_used, :], preferred_element_type=jnp.float32)
        result = both[:, :head_dim] * (1.0 / both[:, head_dim : head_dim + 1])
        result = jnp.where(query_index < length, result, jnp.float32(0.0)).astype(o_ref.dtype)
        for g in range(group):
            o_ref[g, row_start:keys_used, :] = result[g * block : (g + 1) * block]


def attend(heads_first, prompt_kv, length, head_dim, block=256):
    heads, prompt, _ = heads_first.shape
    group = math.gcd(heads, 3)
    grid_spec = pltpu.PrefetchScalarGridSpec(
        num_scalar_prefetch=1,
        grid=(heads // group,),
        in_specs=[
            pl.BlockSpec((group, prompt, head_dim), lambda h, lens: (h, 0, 0)),
            pl.BlockSpec((prompt, 2 * head_dim), lambda h, lens: (0, 0)),
        ],
        out_specs=pl.BlockSpec((group, prompt, head_dim), lambda h, lens: (h, 0, 0)),
        scratch_shapes=[pltpu.VMEM((prompt, 2 * head_dim), jnp.bfloat16)],
    )
    return pl.pallas_call(
        functools.partial(attention_kernel, block, head_dim, group),
        grid_spec=grid_spec,
        out_shape=jax.ShapeDtypeStruct((heads, prompt, head_dim), jnp.bfloat16),
        compiler_params=pltpu.CompilerParams(dimension_semantics=("arbitrary",)),
    )(length, heads_first, prompt_kv)


def per_device(queries, text_kv, image_rows, row_request, row_position, prompt_lengths, kv_weight):
    groups = lax.axis_size("req")
    own_rows = image_rows.shape[0]
    capacity = 2 * own_rows // groups
    prompt = queries.shape[1]
    head_dim = queries.shape[3]
    width = 2 * head_dim
    me = lax.axis_index("tp")
    partial = jnp.einsum("rd,dhc->hrc", image_rows, kv_weight, preferred_element_type=jnp.bfloat16)
    heads = partial.shape[0]
    own_weight = lax.dynamic_index_in_dim(kv_weight, me, axis=1, keepdims=False)
    summed = jnp.dot(image_rows, own_weight, preferred_element_type=jnp.float32)
    for shift in range(1, heads):
        outgoing = lax.dynamic_index_in_dim(partial, (me + shift) % heads, axis=0, keepdims=False)
        incoming = lax.ppermute(
            outgoing, "tp", perm=[(i, (i + shift) % heads) for i in range(heads)]
        )
        summed = summed + incoming.astype(jnp.float32)
    image_kv = rotate_keys(summed, row_position, head_dim)
    one_hot = (row_request[:, None] == jnp.arange(groups, dtype=jnp.int32)[None, :]).astype(
        jnp.int32
    )
    before = jnp.cumsum(one_hot, axis=0) - one_hot
    slot_index = jnp.sum(before * one_hot, axis=1)
    target = row_request * capacity + slot_index
    slots = groups * capacity
    pick = (target[None, :] == jnp.arange(slots, dtype=jnp.int32)[:, None]).astype(jnp.bfloat16)
    send_kv = jnp.dot(pick, image_kv, preferred_element_type=jnp.float32).astype(jnp.bfloat16)
    pos_f = row_position.astype(jnp.float32) + 1.0
    digits = jnp.stack([jnp.floor(pos_f / 16.0), pos_f - 16.0 * jnp.floor(pos_f / 16.0)], axis=1)
    send_pos = jnp.dot(pick.astype(jnp.float32), digits, precision=lax.Precision.HIGHEST)
    tail = send_pos.reshape(groups, 2, capacity).astype(jnp.bfloat16)
    tail = jnp.pad(tail, ((0, 0), (0, 0), (0, 64 - capacity)))
    packet = jnp.concatenate([send_kv.reshape(groups, 2, capacity * width // 2), tail], axis=2)
    got = lax.all_to_all(packet, "req", split_axis=0, concat_axis=0, tiled=True)
    got_kv = got[:, :, : capacity * width // 2].reshape(slots, width)
    got_digits = got[:, :, capacity * width // 2 : capacity * width // 2 + capacity]
    got_digits = got_digits.astype(jnp.int32).reshape(slots, 2)
    places = got_digits[:, 0] * 16 + got_digits[:, 1] - 1
    match = places[None, :] == jnp.arange(prompt, dtype=jnp.int32)[:, None]
    placed = jnp.dot(match.astype(jnp.bfloat16), got_kv, preferred_element_type=jnp.float32)
    hit = jnp.any(match, axis=1)
    prompt_kv = jnp.where(hit[:, None], placed.astype(jnp.bfloat16), text_kv[0, :, 0, :])
    heads_first = jnp.transpose(queries[0], (1, 0, 2))
    out = attend(heads_first, prompt_kv, prompt_lengths, head_dim)
    return jnp.transpose(out, (1, 0, 2))[None]


def solution(mesh):
    in_specs = (
        P("req", None, "tp", None),
        P("req", None, "tp", None),
        P("req", "tp"),
        P("req"),
        P("req"),
        P("req"),
        P("tp", None, None),
    )
    out_specs = P("req", None, "tp", None)
    return jax.shard_map(
        per_device, mesh=mesh, in_specs=in_specs, out_specs=out_specs, check_vma=False
    )
```

```python
import functools
import math

import jax
import jax.numpy as jnp
from jax import lax
from jax.experimental import pallas as pl
from jax.experimental.pallas import tpu as pltpu
from jax.sharding import PartitionSpec as P


def rotate_keys(summed, positions, head_dim):
    half = head_dim // 2
    freqs = jnp.exp(jnp.arange(half, dtype=jnp.float32) * (-2.0 * math.log(1000000.0) / head_dim))
    angles = positions.astype(jnp.float32)[:, None] * freqs[None, :]
    cosine = jnp.cos(angles)
    sine = jnp.sin(angles)
    first = summed[..., :half]
    second = summed[..., half:head_dim]
    rotated = jnp.concatenate(
        [first * cosine - second * sine, second * cosine + first * sine, summed[..., head_dim:]],
        axis=-1,
    )
    return rotated.astype(jnp.bfloat16)


def attention_kernel(block, head_dim, group, len_ref, q_ref, kv_ref, o_ref, vx_ref):
    prompt = q_ref.shape[1]
    length = len_ref[0]
    scale = head_dim ** (-0.5)

    @pl.when(pl.program_id(0) == 0)
    def _():
        vx_ref[:, :head_dim] = kv_ref[:, head_dim:]
        vx_ref[:, head_dim:] = jnp.ones((prompt, head_dim), vx_ref.dtype)

    for index in range(prompt // block):
        row_start = index * block
        keys_used = row_start + block
        query = jnp.concatenate([q_ref[g, row_start:keys_used, :] for g in range(group)], axis=0)
        scores = lax.dot_general(
            query, kv_ref[0:keys_used, 0:head_dim], (((1,), (1,)), ((), ())),
            preferred_element_type=jnp.float32,
        )
        query_index = row_start + lax.broadcasted_iota(jnp.int32, (group * block, 1), 0) % block
        limit = jnp.minimum(query_index, length - 1)
        key_index = row_start + lax.broadcasted_iota(jnp.int32, (1, block), 1)
        diag = jnp.where(key_index <= limit, scores[:, row_start:], jnp.float32(-1e30))
        scores = jnp.concatenate([scores[:, :row_start], diag], axis=1) if row_start else diag
        highest = jnp.max(scores, axis=-1, keepdims=True)
        weights = jnp.exp((scores - highest) * scale).astype(jnp.bfloat16)
        both = jnp.dot(weights, vx_ref[0:keys_used, :], preferred_element_type=jnp.float32)
        result = both[:, :head_dim] / both[:, head_dim : head_dim + 1]
        result = jnp.where(query_index < length, result, jnp.float32(0.0)).astype(o_ref.dtype)
        for g in range(group):
            o_ref[g, row_start:keys_used, :] = result[g * block : (g + 1) * block]


def attend(heads_first, prompt_kv, length, head_dim, block=256):
    heads, prompt, _ = heads_first.shape
    group = math.gcd(heads, 3)
    grid_spec = pltpu.PrefetchScalarGridSpec(
        num_scalar_prefetch=1,
        grid=(heads // group,),
        in_specs=[
            pl.BlockSpec((group, prompt, head_dim), lambda h, lens: (h, 0, 0)),
            pl.BlockSpec((prompt, 2 * head_dim), lambda h, lens: (0, 0)),
        ],
        out_specs=pl.BlockSpec((group, prompt, head_dim), lambda h, lens: (h, 0, 0)),
        scratch_shapes=[pltpu.VMEM((prompt, 2 * head_dim), jnp.bfloat16)],
    )
    return pl.pallas_call(
        functools.partial(attention_kernel, block, head_dim, group),
        grid_spec=grid_spec,
        out_shape=jax.ShapeDtypeStruct((heads, prompt, head_dim), jnp.bfloat16),
        compiler_params=pltpu.CompilerParams(dimension_semantics=("arbitrary",)),
    )(length, heads_first, prompt_kv)


def per_device(queries, text_kv, image_rows, row_request, row_position, prompt_lengths, kv_weight):
    groups = lax.axis_size("req")
    own_rows = image_rows.shape[0]
    capacity = 2 * own_rows // groups
    prompt = queries.shape[1]
    head_dim = queries.shape[3]
    width = 2 * head_dim
    me = lax.axis_index("tp")
    partial = jnp.einsum("rd,dhc->hrc", image_rows, kv_weight, preferred_element_type=jnp.bfloat16)
    heads = partial.shape[0]
    own_weight = lax.dynamic_index_in_dim(kv_weight, me, axis=1, keepdims=False)
    summed = jnp.dot(image_rows, own_weight, preferred_element_type=jnp.float32)
    for shift in range(1, heads):
        outgoing = lax.dynamic_index_in_dim(partial, (me + shift) % heads, axis=0, keepdims=False)
        incoming = lax.ppermute(
            outgoing, "tp", perm=[(i, (i + shift) % heads) for i in range(heads)]
        )
        summed = summed + incoming.astype(jnp.float32)
    image_kv = rotate_keys(summed, row_position, head_dim)
    one_hot = (row_request[:, None] == jnp.arange(groups, dtype=jnp.int32)[None, :]).astype(
        jnp.int32
    )
    before = jnp.cumsum(one_hot, axis=0) - one_hot
    slot_index = jnp.sum(before * one_hot, axis=1)
    target = row_request * capacity + slot_index
    slots = groups * capacity
    pick = (target[None, :] == jnp.arange(slots, dtype=jnp.int32)[:, None]).astype(jnp.bfloat16)
    send_kv = jnp.dot(pick, image_kv, preferred_element_type=jnp.float32).astype(jnp.bfloat16)
    pos_f = row_position.astype(jnp.float32) + 1.0
    digits = jnp.stack([jnp.floor(pos_f / 16.0), pos_f - 16.0 * jnp.floor(pos_f / 16.0)], axis=1)
    send_pos = jnp.dot(pick.astype(jnp.float32), digits, precision=lax.Precision.HIGHEST)
    tail = send_pos.reshape(groups, 2, capacity).astype(jnp.bfloat16)
    tail = jnp.pad(tail, ((0, 0), (0, 0), (0, 64 - capacity)))
    packet = jnp.concatenate([send_kv.reshape(groups, 2, capacity * width // 2), tail], axis=2)
    got = lax.all_to_all(packet, "req", split_axis=0, concat_axis=0, tiled=True)
    got_kv = got[:, :, : capacity * width // 2].reshape(slots, width)
    got_digits = got[:, :, capacity * width // 2 : capacity * width // 2 + capacity]
    got_digits = got_digits.astype(jnp.int32).reshape(slots, 2)
    places = got_digits[:, 0] * 16 + got_digits[:, 1] - 1
    match = places[None, :] == jnp.arange(prompt, dtype=jnp.int32)[:, None]
    placed = jnp.dot(match.astype(jnp.bfloat16), got_kv, preferred_element_type=jnp.float32)
    first = jnp.min(jnp.where(places >= 0, places, prompt))
    last = jnp.max(places)
    spot = jnp.arange(prompt, dtype=jnp.int32)
    hit = (spot >= first) & (spot <= last)
    prompt_kv = jnp.where(hit[:, None], placed.astype(jnp.bfloat16), text_kv[0, :, 0, :])
    heads_first = jnp.transpose(queries[0], (1, 0, 2))
    out = attend(heads_first, prompt_kv, prompt_lengths, head_dim)
    return jnp.transpose(out, (1, 0, 2))[None]


def solution(mesh):
    in_specs = (
        P("req", None, "tp", None),
        P("req", None, "tp", None),
        P("req", "tp"),
        P("req"),
        P("req"),
        P("req"),
        P("tp", None, None),
    )
    out_specs = P("req", None, "tp", None)
    return jax.shard_map(
        per_device, mesh=mesh, in_specs=in_specs, out_specs=out_specs, check_vma=False
    )
```

```python
import functools
import math

import jax
import jax.numpy as jnp
from jax import lax
from jax.experimental import pallas as pl
from jax.experimental.pallas import tpu as pltpu
from jax.sharding import PartitionSpec as P


def rotate_keys(summed, positions, head_dim):
    half = head_dim // 2
    freqs = jnp.exp(jnp.arange(half, dtype=jnp.float32) * (-2.0 * math.log(1000000.0) / head_dim))
    angles = positions.astype(jnp.float32)[:, None] * freqs[None, :]
    cosine = jnp.cos(angles)
    sine = jnp.sin(angles)
    first = summed[..., :half]
    second = summed[..., half:head_dim]
    rotated = jnp.concatenate(
        [first * cosine - second * sine, second * cosine + first * sine, summed[..., head_dim:]],
        axis=-1,
    )
    return rotated.astype(jnp.bfloat16)


def attention_kernel(block, head_dim, group, len_ref, q_ref, kv_ref, o_ref, vx_ref):
    prompt = q_ref.shape[1]
    length = len_ref[0]
    scale = head_dim ** (-0.5)

    @pl.when(pl.program_id(0) == 0)
    def _():
        vx_ref[:, :head_dim] = kv_ref[:, head_dim:]
        vx_ref[:, head_dim:] = jnp.ones((prompt, head_dim), vx_ref.dtype)

    for index in range(prompt // block):
        row_start = index * block
        keys_used = row_start + block
        query = jnp.concatenate([q_ref[g, row_start:keys_used, :] for g in range(group)], axis=0)
        scores = lax.dot_general(
            query, kv_ref[0:keys_used, 0:head_dim], (((1,), (1,)), ((), ())),
            preferred_element_type=jnp.float32,
        )
        query_index = row_start + lax.broadcasted_iota(jnp.int32, (group * block, 1), 0) % block
        limit = jnp.minimum(query_index, length - 1)
        key_index = row_start + lax.broadcasted_iota(jnp.int32, (1, block), 1)
        diag = jnp.where(key_index <= limit, scores[:, row_start:], jnp.float32(-1e30))
        highest = jnp.max(diag, axis=-1, keepdims=True)
        if row_start:
            off = scores[:, :row_start]
            highest = jnp.maximum(highest, jnp.max(off, axis=-1, keepdims=True))
        weights = jnp.exp((diag - highest) * scale).astype(jnp.bfloat16)
        if row_start:
            weights = jnp.concatenate(
                [jnp.exp((off - highest) * scale).astype(jnp.bfloat16), weights], axis=1
            )
        both = jnp.dot(weights, vx_ref[0:keys_used, :], preferred_element_type=jnp.float32)
        result = both[:, :head_dim] / both[:, head_dim : head_dim + 1]
        result = jnp.where(query_index < length, result, jnp.float32(0.0)).astype(o_ref.dtype)
        for g in range(group):
            o_ref[g, row_start:keys_used, :] = result[g * block : (g + 1) * block]


def attend(heads_first, prompt_kv, length, head_dim, block=256):
    heads, prompt, _ = heads_first.shape
    group = math.gcd(heads, 3)
    grid_spec = pltpu.PrefetchScalarGridSpec(
        num_scalar_prefetch=1,
        grid=(heads // group,),
        in_specs=[
            pl.BlockSpec((group, prompt, head_dim), lambda h, lens: (h, 0, 0)),
            pl.BlockSpec((prompt, 2 * head_dim), lambda h, lens: (0, 0)),
        ],
        out_specs=pl.BlockSpec((group, prompt, head_dim), lambda h, lens: (h, 0, 0)),
        scratch_shapes=[pltpu.VMEM((prompt, 2 * head_dim), jnp.bfloat16)],
    )
    return pl.pallas_call(
        functools.partial(attention_kernel, block, head_dim, group),
        grid_spec=grid_spec,
        out_shape=jax.ShapeDtypeStruct((heads, prompt, head_dim), jnp.bfloat16),
        compiler_params=pltpu.CompilerParams(dimension_semantics=("arbitrary",)),
    )(length, heads_first, prompt_kv)


def per_device(queries, text_kv, image_rows, row_request, row_position, prompt_lengths, kv_weight):
    groups = lax.axis_size("req")
    own_rows = image_rows.shape[0]
    capacity = 2 * own_rows // groups
    prompt = queries.shape[1]
    head_dim = queries.shape[3]
    width = 2 * head_dim
    me = lax.axis_index("tp")
    partial = jnp.einsum("rd,dhc->hrc", image_rows, kv_weight, preferred_element_type=jnp.bfloat16)
    heads = partial.shape[0]
    own_weight = lax.dynamic_index_in_dim(kv_weight, me, axis=1, keepdims=False)
    summed = jnp.dot(image_rows, own_weight, preferred_element_type=jnp.float32)
    for shift in range(1, heads):
        outgoing = lax.dynamic_index_in_dim(partial, (me + shift) % heads, axis=0, keepdims=False)
        incoming = lax.ppermute(
            outgoing, "tp", perm=[(i, (i + shift) % heads) for i in range(heads)]
        )
        summed = summed + incoming.astype(jnp.float32)
    image_kv = rotate_keys(summed, row_position, head_dim)
    one_hot = (row_request[:, None] == jnp.arange(groups, dtype=jnp.int32)[None, :]).astype(
        jnp.int32
    )
    before = jnp.cumsum(one_hot, axis=0) - one_hot
    slot_index = jnp.sum(before * one_hot, axis=1)
    target = row_request * capacity + slot_index
    slots = groups * capacity
    pick = (target[None, :] == jnp.arange(slots, dtype=jnp.int32)[:, None]).astype(jnp.bfloat16)
    send_kv = jnp.dot(pick, image_kv, preferred_element_type=jnp.float32).astype(jnp.bfloat16)
    pos_f = row_position.astype(jnp.float32) + 1.0
    digits = jnp.stack([jnp.floor(pos_f / 16.0), pos_f - 16.0 * jnp.floor(pos_f / 16.0)], axis=1)
    send_pos = jnp.dot(pick.astype(jnp.float32), digits, precision=lax.Precision.HIGHEST)
    tail = send_pos.reshape(groups, 2, capacity).astype(jnp.bfloat16)
    tail = jnp.pad(tail, ((0, 0), (0, 0), (0, 64 - capacity)))
    packet = jnp.concatenate([send_kv.reshape(groups, 2, capacity * width // 2), tail], axis=2)
    got = lax.all_to_all(packet, "req", split_axis=0, concat_axis=0, tiled=True)
    got_kv = got[:, :, : capacity * width // 2].reshape(slots, width)
    got_digits = got[:, :, capacity * width // 2 : capacity * width // 2 + capacity]
    got_digits = got_digits.astype(jnp.int32).reshape(slots, 2)
    places = got_digits[:, 0] * 16 + got_digits[:, 1] - 1
    match = places[None, :] == jnp.arange(prompt, dtype=jnp.int32)[:, None]
    placed = jnp.dot(match.astype(jnp.bfloat16), got_kv, preferred_element_type=jnp.float32)
    hit = jnp.any(match, axis=1)
    prompt_kv = jnp.where(hit[:, None], placed.astype(jnp.bfloat16), text_kv[0, :, 0, :])
    heads_first = jnp.transpose(queries[0], (1, 0, 2))
    out = attend(heads_first, prompt_kv, prompt_lengths, head_dim)
    return jnp.transpose(out, (1, 0, 2))[None]


def solution(mesh):
    in_specs = (
        P("req", None, "tp", None),
        P("req", None, "tp", None),
        P("req", "tp"),
        P("req"),
        P("req"),
        P("req"),
        P("tp", None, None),
    )
    out_specs = P("req", None, "tp", None)
    return jax.shard_map(
        per_device, mesh=mesh, in_specs=in_specs, out_specs=out_specs, check_vma=False
    )
```

```python
import functools
import math

import jax
import jax.numpy as jnp
from jax import lax
from jax.experimental import pallas as pl
from jax.experimental.pallas import tpu as pltpu
from jax.sharding import PartitionSpec as P


def rotate_keys(summed, positions, head_dim):
    half = head_dim // 2
    freqs = jnp.exp(jnp.arange(half, dtype=jnp.float32) * (-2.0 * math.log(1000000.0) / head_dim))
    angles = positions.astype(jnp.float32)[:, None] * freqs[None, :]
    cosine = jnp.cos(angles)
    sine = jnp.sin(angles)
    first = summed[..., :half]
    second = summed[..., half:head_dim]
    rotated = jnp.concatenate(
        [first * cosine - second * sine, second * cosine + first * sine, summed[..., head_dim:]],
        axis=-1,
    )
    return rotated.astype(jnp.bfloat16)


def attention_kernel(block, head_dim, group, len_ref, q_ref, kv_ref, o_ref, vx_ref):
    prompt = q_ref.shape[1]
    length = len_ref[0]
    scale = head_dim ** (-0.5)

    @pl.when(pl.program_id(0) == 0)
    def _():
        vx_ref[:, :head_dim] = kv_ref[:, head_dim:]
        vx_ref[:, head_dim:] = jnp.ones((prompt, head_dim), vx_ref.dtype)

    for index in range(prompt // block):
        row_start = index * block
        keys_used = row_start + block
        query = jnp.concatenate([q_ref[g, row_start:keys_used, :] for g in range(group)], axis=0)
        scores = lax.dot_general(
            query, kv_ref[0:keys_used, 0:head_dim], (((1,), (1,)), ((), ())),
            preferred_element_type=jnp.float32,
        )
        query_index = row_start + lax.broadcasted_iota(jnp.int32, (group * block, 1), 0) % block
        limit = jnp.minimum(query_index, length - 1)
        key_index = row_start + lax.broadcasted_iota(jnp.int32, (1, block), 1)
        diag = jnp.where(key_index <= limit, scores[:, row_start:], jnp.float32(-1e30))
        highest = jnp.max(diag, axis=-1, keepdims=True)
        if row_start:
            off = scores[:, :row_start]
            highest = jnp.maximum(highest, jnp.max(off, axis=-1, keepdims=True))
        weights = jnp.exp((diag - highest) * scale).astype(jnp.bfloat16)
        if row_start:
            weights = jnp.concatenate(
                [jnp.exp((off - highest) * scale).astype(jnp.bfloat16), weights], axis=1
            )
        both = jnp.dot(weights, vx_ref[0:keys_used, :], preferred_element_type=jnp.float32)
        result = both[:, :head_dim] * (1.0 / both[:, head_dim : head_dim + 1])
        result = jnp.where(query_index < length, result, jnp.float32(0.0)).astype(o_ref.dtype)
        for g in range(group):
            o_ref[g, row_start:keys_used, :] = result[g * block : (g + 1) * block]


def attend(heads_first, prompt_kv, length, head_dim, block=256):
    heads, prompt, _ = heads_first.shape
    group = math.gcd(heads, 3)
    grid_spec = pltpu.PrefetchScalarGridSpec(
        num_scalar_prefetch=1,
        grid=(heads // group,),
        in_specs=[
            pl.BlockSpec((group, prompt, head_dim), lambda h, lens: (h, 0, 0)),
            pl.BlockSpec((prompt, 2 * head_dim), lambda h, lens: (0, 0)),
        ],
        out_specs=pl.BlockSpec((group, prompt, head_dim), lambda h, lens: (h, 0, 0)),
        scratch_shapes=[pltpu.VMEM((prompt, 2 * head_dim), jnp.bfloat16)],
    )
    return pl.pallas_call(
        functools.partial(attention_kernel, block, head_dim, group),
        grid_spec=grid_spec,
        out_shape=jax.ShapeDtypeStruct((heads, prompt, head_dim), jnp.bfloat16),
        compiler_params=pltpu.CompilerParams(dimension_semantics=("arbitrary",)),
    )(length, heads_first, prompt_kv)


def per_device(queries, text_kv, image_rows, row_request, row_position, prompt_lengths, kv_weight):
    groups = lax.axis_size("req")
    own_rows = image_rows.shape[0]
    capacity = 2 * own_rows // groups
    prompt = queries.shape[1]
    head_dim = queries.shape[3]
    width = 2 * head_dim
    me = lax.axis_index("tp")
    partial = jnp.einsum("rd,dhc->hrc", image_rows, kv_weight, preferred_element_type=jnp.bfloat16)
    heads = partial.shape[0]
    own_weight = lax.dynamic_index_in_dim(kv_weight, me, axis=1, keepdims=False)
    summed = jnp.dot(image_rows, own_weight, preferred_element_type=jnp.float32)
    for shift in range(1, heads):
        outgoing = lax.dynamic_index_in_dim(partial, (me + shift) % heads, axis=0, keepdims=False)
        incoming = lax.ppermute(
            outgoing, "tp", perm=[(i, (i + shift) % heads) for i in range(heads)]
        )
        summed = summed + incoming.astype(jnp.float32)
    image_kv = rotate_keys(summed, row_position, head_dim)
    one_hot = (row_request[:, None] == jnp.arange(groups, dtype=jnp.int32)[None, :]).astype(
        jnp.int32
    )
    before = jnp.cumsum(one_hot, axis=0) - one_hot
    slot_index = jnp.sum(before * one_hot, axis=1)
    target = row_request * capacity + slot_index
    slots = groups * capacity
    pick = (target[None, :] == jnp.arange(slots, dtype=jnp.int32)[:, None]).astype(jnp.bfloat16)
    send_kv = jnp.dot(pick, image_kv, preferred_element_type=jnp.float32).astype(jnp.bfloat16)
    pos_f = row_position.astype(jnp.float32) + 1.0
    digits = jnp.stack([jnp.floor(pos_f / 16.0), pos_f - 16.0 * jnp.floor(pos_f / 16.0)], axis=1)
    send_pos = jnp.dot(pick.astype(jnp.float32), digits, precision=lax.Precision.HIGHEST)
    tail = send_pos.reshape(groups, 2, capacity).astype(jnp.bfloat16)
    tail = jnp.pad(tail, ((0, 0), (0, 0), (0, 64 - capacity)))
    packet = jnp.concatenate([send_kv.reshape(groups, 2, capacity * width // 2), tail], axis=2)
    got = lax.all_to_all(packet, "req", split_axis=0, concat_axis=0, tiled=True)
    got_kv = got[:, :, : capacity * width // 2].reshape(slots, width)
    got_digits = got[:, :, capacity * width // 2 : capacity * width // 2 + capacity]
    got_digits = got_digits.astype(jnp.int32).reshape(slots, 2)
    places = got_digits[:, 0] * 16 + got_digits[:, 1] - 1
    match = places[None, :] == jnp.arange(prompt, dtype=jnp.int32)[:, None]
    placed = jnp.dot(match.astype(jnp.bfloat16), got_kv, preferred_element_type=jnp.float32)
    hit = jnp.any(match, axis=1)
    prompt_kv = jnp.where(hit[:, None], placed.astype(jnp.bfloat16), text_kv[0, :, 0, :])
    heads_first = jnp.transpose(queries[0], (1, 0, 2))
    out = attend(heads_first, prompt_kv, prompt_lengths, head_dim)
    return jnp.transpose(out, (1, 0, 2))[None]


def solution(mesh):
    in_specs = (
        P("req", None, "tp", None),
        P("req", None, "tp", None),
        P("req", "tp"),
        P("req"),
        P("req"),
        P("req"),
        P("tp", None, None),
    )
    out_specs = P("req", None, "tp", None)
    return jax.shard_map(
        per_device, mesh=mesh, in_specs=in_specs, out_specs=out_specs, check_vma=False
    )
```

```python
import functools
import math

import jax
import jax.numpy as jnp
from jax import lax
from jax.experimental import pallas as pl
from jax.experimental.pallas import tpu as pltpu
from jax.sharding import PartitionSpec as P


def rotate_keys(summed, positions, head_dim):
    half = head_dim // 2
    freqs = jnp.exp(jnp.arange(half, dtype=jnp.float32) * (-2.0 * math.log(1000000.0) / head_dim))
    angles = positions.astype(jnp.float32)[:, None] * freqs[None, :]
    cosine = jnp.cos(angles)
    sine = jnp.sin(angles)
    first = summed[..., :half]
    second = summed[..., half:head_dim]
    rotated = jnp.concatenate(
        [first * cosine - second * sine, second * cosine + first * sine, summed[..., head_dim:]],
        axis=-1,
    )
    return rotated.astype(jnp.bfloat16)


def attention_kernel(block, head_dim, group, len_ref, q_ref, kv_ref, o_ref, vx_ref):
    prompt = q_ref.shape[1]
    length = len_ref[0]
    scale = head_dim ** (-0.5)

    @pl.when(pl.program_id(0) == 0)
    def _():
        vx_ref[:, :head_dim] = kv_ref[:, head_dim:]
        vx_ref[:, head_dim:] = jnp.ones((prompt, head_dim), vx_ref.dtype)

    for index in range(prompt // block):
        row_start = index * block
        keys_used = row_start + block
        query = jnp.concatenate([q_ref[g, row_start:keys_used, :] for g in range(group)], axis=0)
        scores = lax.dot_general(
            query, kv_ref[0:keys_used, 0:head_dim], (((1,), (1,)), ((), ())),
            preferred_element_type=jnp.float32,
        )
        query_index = row_start + lax.broadcasted_iota(jnp.int32, (group * block, 1), 0) % block
        limit = jnp.minimum(query_index, length - 1)
        key_index = row_start + lax.broadcasted_iota(jnp.int32, (1, block), 1)
        diag = jnp.where(key_index <= limit, scores[:, row_start:], jnp.float32(-1e30))
        scores = jnp.concatenate([scores[:, :row_start], diag], axis=1) if row_start else diag
        highest = jnp.max(scores, axis=-1, keepdims=True)
        weights = jnp.exp((scores - highest) * scale).astype(jnp.bfloat16)
        both = jnp.dot(weights, vx_ref[0:keys_used, :], preferred_element_type=jnp.float32)
        result = both[:, :head_dim] / both[:, head_dim : head_dim + 1]
        result = jnp.where(query_index < length, result, jnp.float32(0.0)).astype(o_ref.dtype)
        for g in range(group):
            o_ref[g, row_start:keys_used, :] = result[g * block : (g + 1) * block]


def attend(heads_first, prompt_kv, length, head_dim, block=256):
    heads, prompt, _ = heads_first.shape
    group = math.gcd(heads, 6)
    grid_spec = pltpu.PrefetchScalarGridSpec(
        num_scalar_prefetch=1,
        grid=(heads // group,),
        in_specs=[
            pl.BlockSpec((group, prompt, head_dim), lambda h, lens: (h, 0, 0)),
            pl.BlockSpec((prompt, 2 * head_dim), lambda h, lens: (0, 0)),
        ],
        out_specs=pl.BlockSpec((group, prompt, head_dim), lambda h, lens: (h, 0, 0)),
        scratch_shapes=[pltpu.VMEM((prompt, 2 * head_dim), jnp.bfloat16)],
    )
    return pl.pallas_call(
        functools.partial(attention_kernel, block, head_dim, group),
        grid_spec=grid_spec,
        out_shape=jax.ShapeDtypeStruct((heads, prompt, head_dim), jnp.bfloat16),
        compiler_params=pltpu.CompilerParams(dimension_semantics=("arbitrary",)),
    )(length, heads_first, prompt_kv)


def per_device(queries, text_kv, image_rows, row_request, row_position, prompt_lengths, kv_weight):
    groups = lax.axis_size("req")
    own_rows = image_rows.shape[0]
    capacity = 2 * own_rows // groups
    prompt = queries.shape[1]
    head_dim = queries.shape[3]
    width = 2 * head_dim
    me = lax.axis_index("tp")
    partial = jnp.einsum("rd,dhc->hrc", image_rows, kv_weight, preferred_element_type=jnp.bfloat16)
    heads = partial.shape[0]
    own_weight = lax.dynamic_index_in_dim(kv_weight, me, axis=1, keepdims=False)
    summed = jnp.dot(image_rows, own_weight, preferred_element_type=jnp.float32)
    for shift in range(1, heads):
        outgoing = lax.dynamic_index_in_dim(partial, (me + shift) % heads, axis=0, keepdims=False)
        incoming = lax.ppermute(
            outgoing, "tp", perm=[(i, (i + shift) % heads) for i in range(heads)]
        )
        summed = summed + incoming.astype(jnp.float32)
    image_kv = rotate_keys(summed, row_position, head_dim)
    one_hot = (row_request[:, None] == jnp.arange(groups, dtype=jnp.int32)[None, :]).astype(
        jnp.int32
    )
    before = jnp.cumsum(one_hot, axis=0) - one_hot
    slot_index = jnp.sum(before * one_hot, axis=1)
    target = row_request * capacity + slot_index
    slots = groups * capacity
    pick = (target[None, :] == jnp.arange(slots, dtype=jnp.int32)[:, None]).astype(jnp.bfloat16)
    send_kv = jnp.dot(pick, image_kv, preferred_element_type=jnp.float32).astype(jnp.bfloat16)
    pos_f = row_position.astype(jnp.float32) + 1.0
    digits = jnp.stack([jnp.floor(pos_f / 16.0), pos_f - 16.0 * jnp.floor(pos_f / 16.0)], axis=1)
    send_pos = jnp.dot(pick.astype(jnp.float32), digits, precision=lax.Precision.HIGHEST)
    tail = send_pos.reshape(groups, 2, capacity).astype(jnp.bfloat16)
    tail = jnp.pad(tail, ((0, 0), (0, 0), (0, 64 - capacity)))
    packet = jnp.concatenate([send_kv.reshape(groups, 2, capacity * width // 2), tail], axis=2)
    got = lax.all_to_all(packet, "req", split_axis=0, concat_axis=0, tiled=True)
    got_kv = got[:, :, : capacity * width // 2].reshape(slots, width)
    got_digits = got[:, :, capacity * width // 2 : capacity * width // 2 + capacity]
    got_digits = got_digits.astype(jnp.int32).reshape(slots, 2)
    places = got_digits[:, 0] * 16 + got_digits[:, 1] - 1
    match = places[None, :] == jnp.arange(prompt, dtype=jnp.int32)[:, None]
    placed = jnp.dot(match.astype(jnp.bfloat16), got_kv, preferred_element_type=jnp.float32)
    hit = jnp.any(match, axis=1)
    prompt_kv = jnp.where(hit[:, None], placed.astype(jnp.bfloat16), text_kv[0, :, 0, :])
    heads_first = jnp.transpose(queries[0], (1, 0, 2))
    out = attend(heads_first, prompt_kv, prompt_lengths, head_dim)
    return jnp.transpose(out, (1, 0, 2))[None]


def solution(mesh):
    in_specs = (
        P("req", None, "tp", None),
        P("req", None, "tp", None),
        P("req", "tp"),
        P("req"),
        P("req"),
        P("req"),
        P("tp", None, None),
    )
    out_specs = P("req", None, "tp", None)
    return jax.shard_map(
        per_device, mesh=mesh, in_specs=in_specs, out_specs=out_specs, check_vma=False
    )
```
